128 devices in a mesh: quad: 8 (over y, z_lo), area: 16 (over x, z_hi, core).
Axes of the slice: x: 4, y: 4, z: 4 (z_hi: 2, z_lo: 2; z = z_hi * 2 + z_lo), core: 2. Of those that a mesh axis runs over, the one named last changes fastest.
Arguments:
- inverses: bfloat16 [32, 2, 16384, 1024], P('quad', None, 'area'), may hold values from -0.125 to 0.125
- coupling: bfloat16 [16384, 256], P('area'), may hold values from -0.3125 to 0.3125
- probes: bfloat16 [16384, 64], P('area'), may hold values from -6 to 6
- interface_diagonal: float32 [2048], P('area'), may hold values from 2 to 4
- area_rows: int32 [16, 256], replicated, may hold values from 0 to 2047, as said below
- live_counts: int32 [16], P('area'), may hold values from 128 to 256
Outputs:
- interior_moments: float32 [2, 16384, 128], P(None, ('area', 'quad'))
- interface_moments: float32 [2, 2048, 128], P(None, ('area', 'quad'))
The draws below stay inside these ranges and needn't reach their ends.
Inputs may be any that keep to these rules, and one draw needn't show every extreme that they name: `area_rows`: slot s of every area's list holds an interface state owned by area s // 16, that is in [(s // 16) * 128, (s // 16 + 1) * 128); the 256 states of one area's list are distinct.
All inputs are finite; a program needn't handle non-finite values.
Results may differ from the reference program's by a relative error of at most 0.018.
Values may be sent and summed in bfloat16 or wider, within the bound.
No kernel may reach another device: no remote copies, remote signals or barrier semaphores. Data moves between devices by JAX's collectives and lax.ppermute only.
A program may use at most 128 MiB of HBM per device.

```python
import math
import jax
import jax.numpy as jnp
from jax import lax

NI = 1024
P_SIZE = 64
CAP = 16
NG_DEV = 128
ITERS = 4
AREAS = 16
QPTS = 32
GMAX = 256
NG = 2048


def choose_offsets(pair_key):
    return jax.random.permutation(pair_key, NG_DEV)[:CAP].astype(jnp.int32)


def draw_area_rows(key, part):
    pair_keys = jax.random.split(jax.random.fold_in(key, 11), AREAS * AREAS)
    offsets = jax.vmap(choose_offsets)(pair_keys).reshape(AREAS, AREAS, CAP)
    chosen = jax.random.randint(jax.random.fold_in(key, 12), (), 0, AREAS)
    final_block = offsets[:, AREAS - 1, :]
    rotated = (final_block - final_block[:, :1] + NG_DEV - 1) % NG_DEV
    selected = (jnp.arange(AREAS) == chosen)[:, None]
    offsets = offsets.at[:, AREAS - 1, :].set(jnp.where(selected, rotated, final_block))
    block_base = (jnp.arange(AREAS, dtype=jnp.int32) * NG_DEV)[None, :, None]
    return (offsets + block_base).reshape(AREAS, AREAS * CAP).astype(jnp.int32)


def draw_live_counts(key, part):
    counts = jax.random.randint(jax.random.fold_in(key, 21), (AREAS,), GMAX // 2, GMAX + 1)
    shuffled = jax.random.permutation(jax.random.fold_in(key, 22), AREAS)
    counts = counts.at[shuffled[0]].set(GMAX).at[shuffled[1]].set(GMAX // 2)
    return counts.astype(jnp.int32)


def steps_of(rng, dims, shards, low, top_value):
    level, own = 1.0, jax.random.fold_in(rng, 6)
    for position, blocks in shards:
        heights = jnp.exp(jax.random.uniform(jax.random.fold_in(own, position), (blocks,), jnp.float32, low / len(shards), top_value / len(shards)))
        level = level * jnp.repeat(heights, dims[position] // blocks).reshape([-1 if axis == position else 1 for axis in range(len(dims))])
    return level


def noise(key, extent, spread, limit, cuts=(), kind=jnp.bfloat16):
    array = spread * jax.random.normal(key, extent, jnp.float32)
    if cuts:
        array = array * steps_of(key, extent, cuts, -0.22, 0.18)
    return jnp.clip(array, -limit, limit).astype(kind)


def setup_inputs(seed: int = 0) -> dict:
    keys = jax.random.split(jax.random.key(seed), 7)
    inverses = noise(keys[0], (QPTS, 2, AREAS * NI, NI), (2 * NI) ** -0.5, 0.125, ((0, 8), (2, 16)))
    coupling = noise(keys[1], (AREAS * NI, GMAX), (NI * 2 // 5) ** -0.5, 0.3125, ((0, 16),))
    probes = noise(keys[2], (AREAS * NI, P_SIZE), 1.0, 6.0, ((0, 16),))
    interface_diagonal = jnp.clip(2.0 + 2.0 * jax.random.uniform(keys[3], (NG,), jnp.float32) ** steps_of(keys[3], (NG,), ((0, 16),), -0.2, 0.2), 2.0, 4.0)
    area_rows = draw_area_rows(jax.random.fold_in(keys[6], 71), 0)
    live_counts = draw_live_counts(jax.random.fold_in(keys[6], 71), 0)
    return {"inverses": inverses, "coupling": coupling, "probes": probes, "interface_diagonal": interface_diagonal, "area_rows": area_rows, "live_counts": live_counts}


def to_half(values):
    return lax.optimization_barrier(values.astype(jnp.bfloat16)).astype(jnp.float32)


def point_moments(values, angle_now):
    width_half = values.shape[-1] // 2
    value_re = values[..., :width_half]
    value_im = values[..., width_half:]
    results = []
    for power_index in (1, 2):
        cosine_now = jnp.cos(power_index * angle_now)
        sine_now = jnp.sin(power_index * angle_now)
        real_term = cosine_now * value_re - sine_now * value_im
        imag_term = cosine_now * value_im + sine_now * value_re
        results.append(jnp.concatenate([real_term, imag_term], axis=-1))
    return jnp.stack(results)


def reference(inverses, coupling, probes, interface_diagonal, area_rows, live_counts):
    highest = lax.Precision.HIGHEST
    live_mask = (jnp.arange(GMAX)[None, :] < live_counts[:, None]).astype(jnp.float32)
    coupling_live = coupling.astype(jnp.float32).reshape(AREAS, NI, GMAX) * live_mask[:, None, :]
    probe_real = probes.astype(jnp.float32).reshape(AREAS, NI, P_SIZE)
    drive_start = jnp.concatenate([probe_real, jnp.zeros_like(probe_real)], axis=-1)
    flat_rows = area_rows.reshape(-1)
    angle_step = jnp.float32(2.0 * math.pi / QPTS)

    def one_point(moment_carry, point_index):
        angle_now = (point_index.astype(jnp.float32) + 0.5) * angle_step
        shift_re = jnp.cos(angle_now)
        shift_im = jnp.sin(angle_now)
        inverse_now = lax.dynamic_index_in_dim(inverses, point_index, 0, keepdims=False)
        inverse_now = inverse_now.astype(jnp.float32).reshape(2, AREAS, NI, NI)
        interface_values = jnp.zeros((NG, 2 * P_SIZE), jnp.float32)
        states = None
        for sweep_index in range(ITERS + 1):
            sent_values = to_half(interface_values)
            gathered_rows = sent_values[area_rows]
            drive_float = drive_start + jnp.einsum("aig,agc->aic", coupling_live, gathered_rows, precision=highest)
            drive_half = to_half(drive_float)
            swapped = jnp.concatenate([-drive_half[..., P_SIZE:], drive_half[..., :P_SIZE]], axis=-1)
            real_part = jnp.einsum("aij,ajc->aic", inverse_now[0], drive_half, precision=highest)
            imag_part = jnp.einsum("aij,ajc->aic", inverse_now[1], swapped, precision=highest)
            states = real_part + imag_part
            if sweep_index < ITERS:
                replies = jnp.einsum("aig,aic->agc", coupling_live, to_half(states), precision=highest)
                summed = jax.ops.segment_sum(replies.reshape(AREAS * GMAX, 2 * P_SIZE), flat_rows, num_segments=NG)
                real_den = shift_re - interface_diagonal
                imag_den = shift_im * jnp.ones_like(interface_diagonal)
                norm_den = real_den * real_den + imag_den * imag_den
                summed_re = summed[:, :P_SIZE]
                summed_im = summed[:, P_SIZE:]
                new_re = (summed_re * real_den[:, None] + summed_im * imag_den[:, None]) / norm_den[:, None]
                new_im = (summed_im * real_den[:, None] - summed_re * imag_den[:, None]) / norm_den[:, None]
                interface_values = jnp.concatenate([new_re, new_im], axis=-1)
        inner_term = point_moments(states.reshape(AREAS * NI, 2 * P_SIZE), angle_now)
        owned_term = point_moments(interface_values, angle_now)
        return (moment_carry[0] + inner_term, moment_carry[1] + owned_term), None

    start_carry = (jnp.zeros((2, AREAS * NI, 2 * P_SIZE), jnp.float32), jnp.zeros((2, NG, 2 * P_SIZE), jnp.float32))
    final_carry, unused = lax.scan(one_point, start_carry, jnp.arange(QPTS, dtype=jnp.int32))
    return (final_carry[0], final_carry[1])
```

```python
import math

import jax
import jax.numpy as jnp
from jax import lax
from jax.sharding import PartitionSpec as P

ITERS = 4
F32 = jnp.float32
BF16 = jnp.bfloat16


def split_hi_lo(value):
    high = value.astype(BF16)
    low = (value - high.astype(F32)).astype(BF16)
    return high, low


def split_three(value):
    first = value.astype(BF16)
    rest = value - first.astype(F32)
    second = rest.astype(BF16)
    third = (rest - second.astype(F32)).astype(BF16)
    return first, second, third


def dot_split(spec, left_parts, right_parts):
    total = None
    for left in left_parts:
        for right in right_parts:
            term = jnp.einsum(spec, left, right, preferred_element_type=F32)
            total = term if total is None else total + term
    return total


def complex_block(values):
    width_half = values.shape[-1] // 2
    value_re = values[..., :width_half]
    value_im = values[..., width_half:]
    lower = jnp.concatenate([-value_im, value_re], axis=-1)
    return jnp.concatenate([values, lower], axis=-2)


def divide_rows(summed, shift_re, shift_im, diagonal_rows):
    width_half = summed.shape[-1] // 2
    real_den = shift_re[:, None] - diagonal_rows[None, :]
    imag_den = shift_im[:, None] * jnp.ones_like(diagonal_rows)[None, :]
    norm_den = real_den * real_den + imag_den * imag_den
    summed_re = summed[..., :width_half]
    summed_im = summed[..., width_half:]
    new_re = (summed_re * real_den[..., None] + summed_im * imag_den[..., None]) / norm_den[
        ..., None
    ]
    new_im = (summed_im * real_den[..., None] - summed_re * imag_den[..., None]) / norm_den[
        ..., None
    ]
    return jnp.concatenate([new_re, new_im], axis=-1)


def weight_moments(values, angles):
    width_half = values.shape[-1] // 2
    value_re = values[..., :width_half]
    value_im = values[..., width_half:]
    results = []
    for power_index in (1, 2):
        cosine_now = jnp.cos(power_index * angles)[:, None, None]
        sine_now = jnp.sin(power_index * angles)[:, None, None]
        real_term = jnp.sum(cosine_now * value_re - sine_now * value_im, axis=0)
        imag_term = jnp.sum(cosine_now * value_im + sine_now * value_re, axis=0)
        results.append(jnp.concatenate([real_term, imag_term], axis=-1))
    return jnp.stack(results)


def on_device(inverses, coupling, probes, interface_diagonal, area_rows, live_counts):
    local_points = inverses.shape[0]
    area_count = lax.axis_size("area")
    quad_count = lax.axis_size("quad")
    area_index = lax.axis_index("area")
    shared_rows = coupling.shape[1]
    probe_width = probes.shape[1]
    owned_rows = interface_diagonal.shape[0]
    bucket = shared_rows // area_count
    live_mask = jnp.arange(shared_rows) < live_counts[0]
    coupling_live = jnp.where(live_mask[None, :], coupling, jnp.zeros_like(coupling))
    right = jnp.concatenate([probes, coupling_live], axis=1)
    applied = jnp.einsum("qrij,jc->qric", inverses, right, preferred_element_type=F32)
    applied_parts = split_hi_lo(applied)
    projected = dot_split("ig,qric->qrgc", (coupling_live,), applied_parts)
    probe_state = jnp.concatenate(
        [applied[:, 0, :, :probe_width], applied[:, 1, :, :probe_width]], axis=-1
    )
    state_map = jnp.concatenate(
        [applied[:, 0, :, probe_width:], applied[:, 1, :, probe_width:]], axis=-1
    )
    reply_start = jnp.concatenate(
        [projected[:, 0, :, :probe_width], projected[:, 1, :, :probe_width]], axis=-1
    )
    reply_map = jnp.concatenate(
        [projected[:, 0, :, probe_width:], projected[:, 1, :, probe_width:]], axis=-1
    )
    reply_parts = split_hi_lo(reply_map)
    block_offsets = (
        lax.dynamic_slice_in_dim(area_rows, area_index * bucket, bucket, 1)
        - area_index * owned_rows
    )
    flat_offsets = block_offsets.reshape(-1)
    selector = (flat_offsets[None, :] == jnp.arange(owned_rows)[:, None]).astype(BF16)
    angle_step = jnp.float32(2.0 * math.pi / (local_points * quad_count))
    point_ids = lax.axis_index("quad") * local_points + jnp.arange(local_points, dtype=jnp.int32)
    angles = (point_ids.astype(jnp.float32) + 0.5) * angle_step
    shift_re = jnp.cos(angles)
    shift_im = jnp.sin(angles)
    gathered_block = None
    interface_values = None
    for sweep_index in range(ITERS):
        if sweep_index == 0:
            replies = reply_start
        else:
            replies = reply_start + dot_split("qgh,qhc->qgc", reply_parts, (gathered_block,))
        parcels = replies.reshape(local_points, area_count, bucket, 2 * probe_width)
        arrived = lax.all_to_all(parcels, "area", split_axis=1, concat_axis=1, tiled=True)
        arrived = arrived.reshape(local_points, area_count * bucket, 2 * probe_width)
        summed = dot_split("rn,qnc->qrc", (selector,), split_three(arrived))
        interface_values = divide_rows(summed, shift_re, shift_im, interface_diagonal)
        outgoing = jnp.einsum(
            "rn,qrc->qnc",
            selector,
            interface_values.astype(BF16),
            preferred_element_type=F32,
        ).astype(BF16)
        outgoing = outgoing.reshape(local_points, area_count, bucket, 2 * probe_width)
        returned = lax.all_to_all(outgoing, "area", split_axis=1, concat_axis=1, tiled=True)
        gathered_rows = returned.reshape(local_points, shared_rows, 2 * probe_width)
        gathered_block = complex_block(gathered_rows)
    states = probe_state + dot_split("qih,qhc->qic", split_hi_lo(state_map), (gathered_block,))
    inner_moments = lax.psum_scatter(
        weight_moments(states, angles), "quad", scatter_dimension=1, tiled=True
    )
    owned_moments = lax.psum_scatter(
        weight_moments(interface_values, angles), "quad", scatter_dimension=1, tiled=True
    )
    return (inner_moments, owned_moments)


def solution(mesh):
    return jax.shard_map(
        on_device,
        mesh=mesh,
        in_specs=(
            P("quad", None, "area", None),
            P("area", None),
            P("area", None),
            P("area"),
            P(),
            P("area"),
        ),
        out_specs=(P(None, ("area", "quad"), None), P(None, ("area", "quad"), None)),
        check_vma=False,
    )
```

```python
import math

import jax
import jax.numpy as jnp
from jax import lax
from jax.sharding import PartitionSpec as P

ITERS = 4
F32 = jnp.float32
BF16 = jnp.bfloat16


def split_hi_lo(value):
    high = value.astype(BF16)
    low = (value - high.astype(F32)).astype(BF16)
    return high, low


def split_three(value):
    first = value.astype(BF16)
    rest = value - first.astype(F32)
    second = rest.astype(BF16)
    third = (rest - second.astype(F32)).astype(BF16)
    return first, second, third


def dot_split(spec, left_parts, right_parts):
    total = None
    for left in left_parts:
        for right in right_parts:
            term = jnp.einsum(spec, left, right, preferred_element_type=F32)
            total = term if total is None else total + term
    return total


def complex_block(values):
    width_half = values.shape[-1] // 2
    value_re = values[..., :width_half]
    value_im = values[..., width_half:]
    lower = jnp.concatenate([-value_im, value_re], axis=-1)
    return jnp.concatenate([values, lower], axis=-2)


def divide_rows(summed, shift_re, shift_im, diagonal_rows):
    width_half = summed.shape[-1] // 2
    real_den = shift_re[:, None] - diagonal_rows[None, :]
    imag_den = shift_im[:, None] * jnp.ones_like(diagonal_rows)[None, :]
    norm_den = real_den * real_den + imag_den * imag_den
    summed_re = summed[..., :width_half]
    summed_im = summed[..., width_half:]
    new_re = (summed_re * real_den[..., None] + summed_im * imag_den[..., None]) / norm_den[
        ..., None
    ]
    new_im = (summed_im * real_den[..., None] - summed_re * imag_den[..., None]) / norm_den[
        ..., None
    ]
    return jnp.concatenate([new_re, new_im], axis=-1)


def sent_and_summed(value, axis, dim):
    before, after = (value.shape[:dim], value.shape[dim + 1 :])
    parts = jnp.moveaxis(value.reshape(*before, lax.axis_size(axis), -1, *after), dim, 0)
    arrived = lax.all_to_all(parts, axis, split_axis=0, concat_axis=0, tiled=True)
    return arrived.sum(axis=0)


def weight_moments(values, angles):
    width_half = values.shape[-1] // 2
    value_re = values[..., :width_half]
    value_im = values[..., width_half:]
    results = []
    for power_index in (1, 2):
        cosine_now = jnp.cos(power_index * angles)[:, None, None]
        sine_now = jnp.sin(power_index * angles)[:, None, None]
        real_term = jnp.sum(cosine_now * value_re - sine_now * value_im, axis=0)
        imag_term = jnp.sum(cosine_now * value_im + sine_now * value_re, axis=0)
        results.append(jnp.concatenate([real_term, imag_term], axis=-1))
    return jnp.stack(results)


def on_device(inverses, coupling, probes, interface_diagonal, area_rows, live_counts):
    local_points = inverses.shape[0]
    area_count = lax.axis_size("area")
    quad_count = lax.axis_size("quad")
    area_index = lax.axis_index("area")
    shared_rows = coupling.shape[1]
    probe_width = probes.shape[1]
    owned_rows = interface_diagonal.shape[0]
    bucket = shared_rows // area_count
    live_mask = jnp.arange(shared_rows) < live_counts[0]
    coupling_live = jnp.where(live_mask[None, :], coupling, jnp.zeros_like(coupling))
    right = jnp.concatenate([probes, coupling_live], axis=1)
    applied = jnp.einsum("qrij,jc->qric", inverses, right, preferred_element_type=F32)
    applied_parts = split_hi_lo(applied)
    projected = dot_split("ig,qric->qrgc", (coupling_live,), applied_parts)
    probe_state = jnp.concatenate(
        [applied[:, 0, :, :probe_width], applied[:, 1, :, :probe_width]], axis=-1
    )
    state_map = jnp.concatenate(
        [applied[:, 0, :, probe_width:], applied[:, 1, :, probe_width:]], axis=-1
    )
    reply_start = jnp.concatenate(
        [projected[:, 0, :, :probe_width], projected[:, 1, :, :probe_width]], axis=-1
    )
    reply_map = jnp.concatenate(
        [projected[:, 0, :, probe_width:], projected[:, 1, :, probe_width:]], axis=-1
    )
    reply_parts = split_hi_lo(reply_map)
    block_offsets = (
        lax.dynamic_slice_in_dim(area_rows, area_index * bucket, bucket, 1)
        - area_index * owned_rows
    )
    flat_offsets = block_offsets.reshape(-1)
    selector = (flat_offsets[None, :] == jnp.arange(owned_rows)[:, None]).astype(BF16)
    angle_step = jnp.float32(2.0 * math.pi / (local_points * quad_count))
    point_ids = lax.axis_index("quad") * local_points + jnp.arange(local_points, dtype=jnp.int32)
    angles = (point_ids.astype(jnp.float32) + 0.5) * angle_step
    shift_re = jnp.cos(angles)
    shift_im = jnp.sin(angles)
    gathered_block = None
    interface_values = None
    for sweep_index in range(ITERS):
        if sweep_index == 0:
            replies = reply_start
        else:
            replies = reply_start + dot_split("qgh,qhc->qgc", reply_parts, (gathered_block,))
        parcels = replies.reshape(local_points, area_count, bucket, 2 * probe_width)
        arrived = lax.all_to_all(parcels, "area", split_axis=1, concat_axis=1, tiled=True)
        arrived = arrived.reshape(local_points, area_count * bucket, 2 * probe_width)
        summed = dot_split("rn,qnc->qrc", (selector,), split_three(arrived))
        interface_values = divide_rows(summed, shift_re, shift_im, interface_diagonal)
        outgoing = jnp.einsum(
            "rn,qrc->qnc",
            selector,
            interface_values.astype(BF16),
            preferred_element_type=F32,
        ).astype(BF16)
        outgoing = outgoing.reshape(local_points, area_count, bucket, 2 * probe_width)
        returned = lax.all_to_all(outgoing, "area", split_axis=1, concat_axis=1, tiled=True)
        gathered_rows = returned.reshape(local_points, shared_rows, 2 * probe_width)
        gathered_block = complex_block(gathered_rows)
    states = probe_state + dot_split("qih,qhc->qic", split_hi_lo(state_map), (gathered_block,))
    inner_moments = sent_and_summed(weight_moments(states, angles), "quad", 1)
    owned_moments = sent_and_summed(weight_moments(interface_values, angles), "quad", 1)
    return (inner_moments, owned_moments)


def solution(mesh):
    return jax.shard_map(
        on_device,
        mesh=mesh,
        in_specs=(
            P("quad", None, "area", None),
            P("area", None),
            P("area", None),
            P("area"),
            P(),
            P("area"),
        ),
        out_specs=(P(None, ("area", "quad"), None), P(None, ("area", "quad"), None)),
        check_vma=False,
    )
```

```python
import math

import jax
import jax.numpy as jnp
from jax import lax
from jax.sharding import PartitionSpec as P

ITERS = 4
F32 = jnp.float32
BF16 = jnp.bfloat16


def split_hi_lo(value):
    high = value.astype(BF16)
    low = (value - high.astype(F32)).astype(BF16)
    return high, low


def split_three(value):
    first = value.astype(BF16)
    rest = value - first.astype(F32)
    second = rest.astype(BF16)
    third = (rest - second.astype(F32)).astype(BF16)
    return first, second, third


def dot_split(spec, left_parts, right_parts):
    total = None
    for left in left_parts:
        for right in right_parts:
            term = jnp.einsum(spec, left, right, preferred_element_type=F32)
            total = term if total is None else total + term
    return total


def complex_block(values):
    width_half = values.shape[-1] // 2
    value_re = values[..., :width_half]
    value_im = values[..., width_half:]
    lower = jnp.concatenate([-value_im, value_re], axis=-1)
    return jnp.concatenate([values, lower], axis=-2)


def divide_rows(summed, shift_re, shift_im, diagonal_rows):
    width_half = summed.shape[-1] // 2
    real_den = shift_re[:, None] - diagonal_rows[None, :]
    imag_den = shift_im[:, None] * jnp.ones_like(diagonal_rows)[None, :]
    norm_den = real_den * real_den + imag_den * imag_den
    summed_re = summed[..., :width_half]
    summed_im = summed[..., width_half:]
    new_re = (summed_re * real_den[..., None] + summed_im * imag_den[..., None]) / norm_den[
        ..., None
    ]
    new_im = (summed_im * real_den[..., None] - summed_re * imag_den[..., None]) / norm_den[
        ..., None
    ]
    return jnp.concatenate([new_re, new_im], axis=-1)


def sent_and_summed(value, axis, dim):
    before, after = (value.shape[:dim], value.shape[dim + 1 :])
    parts = jnp.moveaxis(value.reshape(*before, lax.axis_size(axis), -1, *after), dim, 0)
    arrived = lax.all_to_all(parts, axis, split_axis=0, concat_axis=0, tiled=True)
    return arrived.sum(axis=0)


def weight_moments(values, angles):
    width_half = values.shape[-1] // 2
    value_re = values[..., :width_half]
    value_im = values[..., width_half:]
    results = []
    for power_index in (1, 2):
        cosine_now = jnp.cos(power_index * angles)[:, None, None]
        sine_now = jnp.sin(power_index * angles)[:, None, None]
        real_term = jnp.sum(cosine_now * value_re - sine_now * value_im, axis=0)
        imag_term = jnp.sum(cosine_now * value_im + sine_now * value_re, axis=0)
        results.append(jnp.concatenate([real_term, imag_term], axis=-1))
    return jnp.stack(results)


def on_device(inverses, coupling, probes, interface_diagonal, area_rows, live_counts):
    local_points = inverses.shape[0]
    area_count = lax.axis_size("area")
    quad_count = lax.axis_size("quad")
    area_index = lax.axis_index("area")
    shared_rows = coupling.shape[1]
    probe_width = probes.shape[1]
    owned_rows = interface_diagonal.shape[0]
    bucket = shared_rows // area_count
    live_mask = jnp.arange(shared_rows) < live_counts[0]
    coupling_live = jnp.where(live_mask[None, :], coupling, jnp.zeros_like(coupling))
    applied_probe = jnp.einsum("qrij,jc->qric", inverses, probes, preferred_element_type=F32)
    applied_map = jnp.einsum("qrij,jc->qric", inverses, coupling_live, preferred_element_type=F32)
    projected_probe = dot_split("ig,qric->qrgc", (coupling_live,), split_hi_lo(applied_probe))
    projected_map = dot_split("ig,qric->qrgc", (coupling_live,), split_hi_lo(applied_map))
    probe_state = jnp.concatenate([applied_probe[:, 0], applied_probe[:, 1]], axis=-1)
    state_map = jnp.concatenate([applied_map[:, 0], applied_map[:, 1]], axis=-1)
    reply_start = jnp.concatenate([projected_probe[:, 0], projected_probe[:, 1]], axis=-1)
    reply_map = jnp.concatenate([projected_map[:, 0], projected_map[:, 1]], axis=-1)
    reply_parts = split_hi_lo(reply_map)
    block_offsets = (
        lax.dynamic_slice_in_dim(area_rows, area_index * bucket, bucket, 1)
        - area_index * owned_rows
    )
    flat_offsets = block_offsets.reshape(-1)
    selector = (flat_offsets[None, :] == jnp.arange(owned_rows)[:, None]).astype(BF16)
    angle_step = jnp.float32(2.0 * math.pi / (local_points * quad_count))
    point_ids = lax.axis_index("quad") * local_points + jnp.arange(local_points, dtype=jnp.int32)
    angles = (point_ids.astype(jnp.float32) + 0.5) * angle_step
    shift_re = jnp.cos(angles)
    shift_im = jnp.sin(angles)
    gathered_block = None
    interface_values = None
    for sweep_index in range(ITERS):
        if sweep_index == 0:
            replies = reply_start
        else:
            replies = reply_start + dot_split("qgh,qhc->qgc", reply_parts, (gathered_block,))
        parcels = replies.reshape(local_points, area_count, bucket, 2 * probe_width).astype(BF16)
        arrived = lax.all_to_all(parcels, "area", split_axis=1, concat_axis=1, tiled=True)
        arrived = arrived.reshape(local_points, area_count * bucket, 2 * probe_width)
        summed = jnp.einsum("rn,qnc->qrc", selector, arrived, preferred_element_type=F32)
        interface_values = divide_rows(summed, shift_re, shift_im, interface_diagonal)
        outgoing = jnp.einsum(
            "rn,qrc->qnc",
            selector,
            interface_values.astype(BF16),
            preferred_element_type=F32,
        ).astype(BF16)
        outgoing = outgoing.reshape(local_points, area_count, bucket, 2 * probe_width)
        returned = lax.all_to_all(outgoing, "area", split_axis=1, concat_axis=1, tiled=True)
        gathered_rows = returned.reshape(local_points, shared_rows, 2 * probe_width)
        gathered_block = complex_block(gathered_rows)
    states = probe_state + dot_split("qih,qhc->qic", split_hi_lo(state_map), (gathered_block,))
    inner_moments = sent_and_summed(weight_moments(states, angles), "quad", 1)
    owned_moments = sent_and_summed(weight_moments(interface_values, angles), "quad", 1)
    return (inner_moments, owned_moments)


def solution(mesh):
    return jax.shard_map(
        on_device,
        mesh=mesh,
        in_specs=(
            P("quad", None, "area", None),
            P("area", None),
            P("area", None),
            P("area"),
            P(),
            P("area"),
        ),
        out_specs=(P(None, ("area", "quad"), None), P(None, ("area", "quad"), None)),
        check_vma=False,
    )
```

```python
import math

import jax
import jax.numpy as jnp
from jax import lax
from jax.sharding import PartitionSpec as P

ITERS = 4
F32 = jnp.float32
BF16 = jnp.bfloat16


def split_hi_lo(value):
    high = value.astype(BF16)
    low = (value - high.astype(F32)).astype(BF16)
    return high, low


def split_three(value):
    first = value.astype(BF16)
    rest = value - first.astype(F32)
    second = rest.astype(BF16)
    third = (rest - second.astype(F32)).astype(BF16)
    return first, second, third


def dot_split(spec, left_parts, right_parts):
    total = None
    for left in left_parts:
        for right in right_parts:
            term = jnp.einsum(spec, left, right, preferred_element_type=F32)
            total = term if total is None else total + term
    return total


def complex_block(values):
    width_half = values.shape[-1] // 2
    value_re = values[..., :width_half]
    value_im = values[..., width_half:]
    lower = jnp.concatenate([-value_im, value_re], axis=-1)
    return jnp.concatenate([values, lower], axis=-2)


def divide_rows(summed, shift_re, shift_im, diagonal_rows):
    width_half = summed.shape[-1] // 2
    real_den = shift_re[:, None] - diagonal_rows[None, :]
    imag_den = shift_im[:, None] * jnp.ones_like(diagonal_rows)[None, :]
    norm_den = real_den * real_den + imag_den * imag_den
    summed_re = summed[..., :width_half]
    summed_im = summed[..., width_half:]
    new_re = (summed_re * real_den[..., None] + summed_im * imag_den[..., None]) / norm_den[
        ..., None
    ]
    new_im = (summed_im * real_den[..., None] - summed_re * imag_den[..., None]) / norm_den[
        ..., None
    ]
    return jnp.concatenate([new_re, new_im], axis=-1)


def sent_and_summed(value, axis, dim):
    before, after = (value.shape[:dim], value.shape[dim + 1 :])
    parts = jnp.moveaxis(value.reshape(*before, lax.axis_size(axis), -1, *after), dim, 0)
    arrived = lax.all_to_all(parts, axis, split_axis=0, concat_axis=0, tiled=True)
    return arrived.sum(axis=0)


def weight_moments(values, angles):
    width_half = values.shape[-1] // 2
    value_re = values[..., :width_half]
    value_im = values[..., width_half:]
    results = []
    for power_index in (1, 2):
        cosine_now = jnp.cos(power_index * angles)[:, None, None]
        sine_now = jnp.sin(power_index * angles)[:, None, None]
        real_term = jnp.sum(cosine_now * value_re - sine_now * value_im, axis=0)
        imag_term = jnp.sum(cosine_now * value_im + sine_now * value_re, axis=0)
        results.append(jnp.concatenate([real_term, imag_term], axis=-1))
    return jnp.stack(results)


def on_device(inverses, coupling, probes, interface_diagonal, area_rows, live_counts):
    local_points = inverses.shape[0]
    area_count = lax.axis_size("area")
    quad_count = lax.axis_size("quad")
    area_index = lax.axis_index("area")
    shared_rows = coupling.shape[1]
    probe_width = probes.shape[1]
    owned_rows = interface_diagonal.shape[0]
    bucket = shared_rows // area_count
    live_mask = jnp.arange(shared_rows) < live_counts[0]
    coupling_live = jnp.where(live_mask[None, :], coupling, jnp.zeros_like(coupling))
    right = jnp.concatenate([probes, coupling_live], axis=1)
    applied = jnp.einsum("qrij,jc->qric", inverses, right, preferred_element_type=F32)
    applied_parts = split_hi_lo(applied)
    projected = dot_split("ig,qric->qrgc", (coupling_live,), applied_parts)
    probe_state = jnp.concatenate(
        [applied[:, 0, :, :probe_width], applied[:, 1, :, :probe_width]], axis=-1
    )
    state_map = jnp.concatenate(
        [applied[:, 0, :, probe_width:], applied[:, 1, :, probe_width:]], axis=-1
    )
    reply_start = jnp.concatenate(
        [projected[:, 0, :, :probe_width], projected[:, 1, :, :probe_width]], axis=-1
    )
    reply_map = jnp.concatenate(
        [projected[:, 0, :, probe_width:], projected[:, 1, :, probe_width:]], axis=-1
    )
    reply_parts = split_hi_lo(reply_map)
    block_offsets = (
        lax.dynamic_slice_in_dim(area_rows, area_index * bucket, bucket, 1)
        - area_index * owned_rows
    )
    flat_offsets = block_offsets.reshape(-1)
    selector = (flat_offsets[None, :] == jnp.arange(owned_rows)[:, None]).astype(BF16)
    angle_step = jnp.float32(2.0 * math.pi / (local_points * quad_count))
    point_ids = lax.axis_index("quad") * local_points + jnp.arange(local_points, dtype=jnp.int32)
    angles = (point_ids.astype(jnp.float32) + 0.5) * angle_step
    shift_re = jnp.cos(angles)
    shift_im = jnp.sin(angles)
    gathered_block = None
    interface_values = None
    for sweep_index in range(ITERS):
        if sweep_index == 0:
            replies = reply_start
        else:
            replies = reply_start + dot_split("qgh,qhc->qgc", reply_parts, (gathered_block,))
        parcels = replies.reshape(local_points, area_count, bucket, 2 * probe_width).astype(BF16)
        arrived = lax.all_to_all(parcels, "area", split_axis=1, concat_axis=1, tiled=True)
        arrived = arrived.reshape(local_points, area_count * bucket, 2 * probe_width)
        summed = jnp.einsum("rn,qnc->qrc", selector, arrived, preferred_element_type=F32)
        interface_values = divide_rows(summed, shift_re, shift_im, interface_diagonal)
        outgoing = jnp.einsum(
            "rn,qrc->qnc",
            selector,
            interface_values.astype(BF16),
            preferred_element_type=F32,
        ).astype(BF16)
        outgoing = outgoing.reshape(local_points, area_count, bucket, 2 * probe_width)
        returned = lax.all_to_all(outgoing, "area", split_axis=1, concat_axis=1, tiled=True)
        gathered_rows = returned.reshape(local_points, shared_rows, 2 * probe_width)
        gathered_block = complex_block(gathered_rows)
    states = probe_state + dot_split("qih,qhc->qic", split_hi_lo(state_map), (gathered_block,))
    inner_rows = states.shape[1]
    inner_terms = weight_moments(states, angles)
    owned_terms = weight_moments(interface_values, angles)
    inner_parts = jnp.moveaxis(
        inner_terms.reshape(2, quad_count, inner_rows // quad_count, 2 * probe_width), 1, 0
    )
    owned_parts = jnp.moveaxis(
        owned_terms.reshape(2, quad_count, owned_rows // quad_count, 2 * probe_width), 1, 0
    )
    both = jnp.concatenate([inner_parts, owned_parts], axis=2).astype(BF16)
    summed_both = lax.all_to_all(both, "quad", split_axis=0, concat_axis=0, tiled=True)
    summed_both = summed_both.astype(F32).sum(axis=0)
    inner_moments = summed_both[:, : inner_rows // quad_count]
    owned_moments = summed_both[:, inner_rows // quad_count :]
    return (inner_moments, owned_moments)


def solution(mesh):
    return jax.shard_map(
        on_device,
        mesh=mesh,
        in_specs=(
            P("quad", None, "area", None),
            P("area", None),
            P("area", None),
            P("area"),
            P(),
            P("area"),
        ),
        out_specs=(P(None, ("area", "quad"), None), P(None, ("area", "quad"), None)),
        check_vma=False,
    )
```

```python
import math

import jax
import jax.numpy as jnp
from jax import lax
from jax.sharding import PartitionSpec as P

ITERS = 4
F32 = jnp.float32
BF16 = jnp.bfloat16


def split_hi_lo(value):
    high = value.astype(BF16)
    low = (value - high.astype(F32)).astype(BF16)
    return high, low


def split_three(value):
    first = value.astype(BF16)
    rest = value - first.astype(F32)
    second = rest.astype(BF16)
    third = (rest - second.astype(F32)).astype(BF16)
    return first, second, third


def dot_split(spec, left_parts, right_parts):
    total = None
    for left in left_parts:
        for right in right_parts:
            term = jnp.einsum(spec, left, right, preferred_element_type=F32)
            total = term if total is None else total + term
    return total


def complex_block(values):
    width_half = values.shape[-1] // 2
    value_re = values[..., :width_half]
    value_im = values[..., width_half:]
    lower = jnp.concatenate([-value_im, value_re], axis=-1)
    return jnp.concatenate([values, lower], axis=-2)


def divide_rows(summed, shift_re, shift_im, diagonal_rows):
    width_half = summed.shape[-1] // 2
    real_den = shift_re[:, None] - diagonal_rows[None, :]
    imag_den = shift_im[:, None] * jnp.ones_like(diagonal_rows)[None, :]
    norm_den = real_den * real_den + imag_den * imag_den
    summed_re = summed[..., :width_half]
    summed_im = summed[..., width_half:]
    new_re = (summed_re * real_den[..., None] + summed_im * imag_den[..., None]) / norm_den[
        ..., None
    ]
    new_im = (summed_im * real_den[..., None] - summed_re * imag_den[..., None]) / norm_den[
        ..., None
    ]
    return jnp.concatenate([new_re, new_im], axis=-1)


def sent_and_summed(value, axis, dim):
    before, after = (value.shape[:dim], value.shape[dim + 1 :])
    parts = jnp.moveaxis(value.reshape(*before, lax.axis_size(axis), -1, *after), dim, 0)
    arrived = lax.all_to_all(parts, axis, split_axis=0, concat_axis=0, tiled=True)
    return arrived.sum(axis=0)


def weight_moments(values, angles):
    width_half = values.shape[-1] // 2
    value_re = values[..., :width_half]
    value_im = values[..., width_half:]
    results = []
    for power_index in (1, 2):
        cosine_now = jnp.cos(power_index * angles)[:, None, None]
        sine_now = jnp.sin(power_index * angles)[:, None, None]
        real_term = jnp.sum(cosine_now * value_re - sine_now * value_im, axis=0)
        imag_term = jnp.sum(cosine_now * value_im + sine_now * value_re, axis=0)
        results.append(jnp.concatenate([real_term, imag_term], axis=-1))
    return jnp.stack(results)


def on_device(inverses, coupling, probes, interface_diagonal, area_rows, live_counts):
    local_points = inverses.shape[0]
    area_count = lax.axis_size("area")
    quad_count = lax.axis_size("quad")
    area_index = lax.axis_index("area")
    shared_rows = coupling.shape[1]
    probe_width = probes.shape[1]
    owned_rows = interface_diagonal.shape[0]
    bucket = shared_rows // area_count
    live_mask = jnp.arange(shared_rows) < live_counts[0]
    coupling_live = jnp.where(live_mask[None, :], coupling, jnp.zeros_like(coupling))
    right = jnp.concatenate([probes, coupling_live], axis=1)
    applied = jnp.einsum("qrij,jc->qric", inverses, right, preferred_element_type=F32)
    projected_probe = dot_split(
        "ig,qric->qrgc", (coupling_live,), split_hi_lo(applied[..., :probe_width])
    )
    projected_map = dot_split(
        "ig,qric->qrgc", (coupling_live,), split_hi_lo(applied[..., probe_width:])
    )
    probe_state = jnp.concatenate(
        [applied[:, 0, :, :probe_width], applied[:, 1, :, :probe_width]], axis=-1
    )
    state_map = jnp.concatenate(
        [applied[:, 0, :, probe_width:], applied[:, 1, :, probe_width:]], axis=-1
    )
    reply_start = jnp.concatenate([projected_probe[:, 0], projected_probe[:, 1]], axis=-1)
    reply_map = jnp.concatenate([projected_map[:, 0], projected_map[:, 1]], axis=-1)
    reply_parts = split_hi_lo(reply_map)
    block_offsets = (
        lax.dynamic_slice_in_dim(area_rows, area_index * bucket, bucket, 1)
        - area_index * owned_rows
    )
    flat_offsets = block_offsets.reshape(-1)
    selector = (flat_offsets[None, :] == jnp.arange(owned_rows)[:, None]).astype(BF16)
    angle_step = jnp.float32(2.0 * math.pi / (local_points * quad_count))
    point_ids = lax.axis_index("quad") * local_points + jnp.arange(local_points, dtype=jnp.int32)
    angles = (point_ids.astype(jnp.float32) + 0.5) * angle_step
    shift_re = jnp.cos(angles)
    shift_im = jnp.sin(angles)
    gathered_block = None
    interface_values = None
    for sweep_index in range(ITERS):
        if sweep_index == 0:
            replies = reply_start
        else:
            replies = reply_start + dot_split("qgh,qhc->qgc", reply_parts, (gathered_block,))
        parcels = replies.reshape(local_points, area_count, bucket, 2 * probe_width).astype(BF16)
        arrived = lax.all_to_all(parcels, "area", split_axis=1, concat_axis=1, tiled=True)
        arrived = arrived.reshape(local_points, area_count * bucket, 2 * probe_width)
        summed = jnp.einsum("rn,qnc->qrc", selector, arrived, preferred_element_type=F32)
        interface_values = divide_rows(summed, shift_re, shift_im, interface_diagonal)
        outgoing = jnp.einsum(
            "rn,qrc->qnc",
            selector,
            interface_values.astype(BF16),
            preferred_element_type=F32,
        ).astype(BF16)
        outgoing = outgoing.reshape(local_points, area_count, bucket, 2 * probe_width)
        returned = lax.all_to_all(outgoing, "area", split_axis=1, concat_axis=1, tiled=True)
        gathered_rows = returned.reshape(local_points, shared_rows, 2 * probe_width)
        gathered_block = complex_block(gathered_rows)
    states = probe_state + dot_split("qih,qhc->qic", split_hi_lo(state_map), (gathered_block,))
    inner_rows = states.shape[1]
    inner_terms = weight_moments(states, angles)
    owned_terms = weight_moments(interface_values, angles)
    inner_parts = jnp.moveaxis(
        inner_terms.reshape(2, quad_count, inner_rows // quad_count, 2 * probe_width), 1, 0
    )
    owned_parts = jnp.moveaxis(
        owned_terms.reshape(2, quad_count, owned_rows // quad_count, 2 * probe_width), 1, 0
    )
    both = jnp.concatenate([inner_parts, owned_parts], axis=2).astype(BF16)
    summed_both = lax.all_to_all(both, "quad", split_axis=0, concat_axis=0, tiled=True)
    summed_both = summed_both.astype(F32).sum(axis=0)
    inner_moments = summed_both[:, : inner_rows // quad_count]
    owned_moments = summed_both[:, inner_rows // quad_count :]
    return (inner_moments, owned_moments)


def solution(mesh):
    return jax.shard_map(
        on_device,
        mesh=mesh,
        in_specs=(
            P("quad", None, "area", None),
            P("area", None),
            P("area", None),
            P("area"),
            P(),
            P("area"),
        ),
        out_specs=(P(None, ("area", "quad"), None), P(None, ("area", "quad"), None)),
        check_vma=False,
    )
```

```python
import math

import jax
import jax.numpy as jnp
from jax import lax
from jax.sharding import PartitionSpec as P

ITERS = 4
F32 = jnp.float32
BF16 = jnp.bfloat16


def split_hi_lo(value):
    high = value.astype(BF16)
    low = (value - high.astype(F32)).astype(BF16)
    return high, low


def split_three(value):
    first = value.astype(BF16)
    rest = value - first.astype(F32)
    second = rest.astype(BF16)
    third = (rest - second.astype(F32)).astype(BF16)
    return first, second, third


def dot_split(spec, left_parts, right_parts):
    total = None
    for left in left_parts:
        for right in right_parts:
            term = jnp.einsum(spec, left, right, preferred_element_type=F32)
            total = term if total is None else total + term
    return total


def complex_block(values):
    width_half = values.shape[-1] // 2
    value_re = values[..., :width_half]
    value_im = values[..., width_half:]
    lower = jnp.concatenate([-value_im, value_re], axis=-1)
    return jnp.concatenate([values, lower], axis=-2)


def divide_rows(summed, shift_re, shift_im, diagonal_rows):
    width_half = summed.shape[-1] // 2
    real_den = shift_re[:, None] - diagonal_rows[None, :]
    imag_den = shift_im[:, None] * jnp.ones_like(diagonal_rows)[None, :]
    norm_den = real_den * real_den + imag_den * imag_den
    summed_re = summed[..., :width_half]
    summed_im = summed[..., width_half:]
    new_re = (summed_re * real_den[..., None] + summed_im * imag_den[..., None]) / norm_den[
        ..., None
    ]
    new_im = (summed_im * real_den[..., None] - summed_re * imag_den[..., None]) / norm_den[
        ..., None
    ]
    return jnp.concatenate([new_re, new_im], axis=-1)


def sent_and_summed(value, axis, dim):
    before, after = (value.shape[:dim], value.shape[dim + 1 :])
    parts = jnp.moveaxis(value.reshape(*before, lax.axis_size(axis), -1, *after), dim, 0)
    arrived = lax.all_to_all(parts, axis, split_axis=0, concat_axis=0, tiled=True)
    return arrived.sum(axis=0)


def weight_moments(values, angles):
    width_half = values.shape[-1] // 2
    value_re = values[..., :width_half]
    value_im = values[..., width_half:]
    results = []
    for power_index in (1, 2):
        cosine_now = jnp.cos(power_index * angles)[:, None, None]
        sine_now = jnp.sin(power_index * angles)[:, None, None]
        real_term = jnp.sum(cosine_now * value_re - sine_now * value_im, axis=0)
        imag_term = jnp.sum(cosine_now * value_im + sine_now * value_re, axis=0)
        results.append(jnp.concatenate([real_term, imag_term], axis=-1))
    return jnp.stack(results)


def on_device(inverses, coupling, probes, interface_diagonal, area_rows, live_counts):
    local_points = inverses.shape[0]
    area_count = lax.axis_size("area")
    quad_count = lax.axis_size("quad")
    area_index = lax.axis_index("area")
    shared_rows = coupling.shape[1]
    probe_width = probes.shape[1]
    owned_rows = interface_diagonal.shape[0]
    bucket = shared_rows // area_count
    live_mask = jnp.arange(shared_rows) < live_counts[0]
    coupling_live = jnp.where(live_mask[None, :], coupling, jnp.zeros_like(coupling))
    right = jnp.concatenate([probes, coupling_live], axis=1)
    applied = jnp.einsum("qrij,jc->qric", inverses, right, preferred_element_type=F32)
    projected = jnp.einsum(
        "ig,qric->qrgc", coupling_live, applied.astype(BF16), preferred_element_type=F32
    )
    probe_state = jnp.concatenate(
        [applied[:, 0, :, :probe_width], applied[:, 1, :, :probe_width]], axis=-1
    )
    state_map = jnp.concatenate(
        [applied[:, 0, :, probe_width:], applied[:, 1, :, probe_width:]], axis=-1
    )
    reply_start = jnp.concatenate(
        [projected[:, 0, :, :probe_width], projected[:, 1, :, :probe_width]], axis=-1
    )
    reply_map = jnp.concatenate(
        [projected[:, 0, :, probe_width:], projected[:, 1, :, probe_width:]], axis=-1
    )
    reply_parts = split_hi_lo(reply_map)
    block_offsets = (
        lax.dynamic_slice_in_dim(area_rows, area_index * bucket, bucket, 1)
        - area_index * owned_rows
    )
    flat_offsets = block_offsets.reshape(-1)
    selector = (flat_offsets[None, :] == jnp.arange(owned_rows)[:, None]).astype(BF16)
    angle_step = jnp.float32(2.0 * math.pi / (local_points * quad_count))
    point_ids = lax.axis_index("quad") * local_points + jnp.arange(local_points, dtype=jnp.int32)
    angles = (point_ids.astype(jnp.float32) + 0.5) * angle_step
    shift_re = jnp.cos(angles)
    shift_im = jnp.sin(angles)
    gathered_block = None
    interface_values = None
    for sweep_index in range(ITERS):
        if sweep_index == 0:
            replies = reply_start
        else:
            replies = reply_start + dot_split("qgh,qhc->qgc", reply_parts, (gathered_block,))
        parcels = replies.reshape(local_points, area_count, bucket, 2 * probe_width).astype(BF16)
        arrived = lax.all_to_all(parcels, "area", split_axis=1, concat_axis=1, tiled=True)
        arrived = arrived.reshape(local_points, area_count * bucket, 2 * probe_width)
        summed = jnp.einsum("rn,qnc->qrc", selector, arrived, preferred_element_type=F32)
        interface_values = divide_rows(summed, shift_re, shift_im, interface_diagonal)
        outgoing = jnp.einsum(
            "rn,qrc->qnc",
            selector,
            interface_values.astype(BF16),
            preferred_element_type=F32,
        ).astype(BF16)
        outgoing = outgoing.reshape(local_points, area_count, bucket, 2 * probe_width)
        returned = lax.all_to_all(outgoing, "area", split_axis=1, concat_axis=1, tiled=True)
        gathered_rows = returned.reshape(local_points, shared_rows, 2 * probe_width)
        gathered_block = complex_block(gathered_rows)
    states = probe_state + jnp.einsum(
        "qih,qhc->qic", state_map.astype(BF16), gathered_block, preferred_element_type=F32
    )
    inner_rows = states.shape[1]
    inner_terms = weight_moments(states, angles)
    owned_terms = weight_moments(interface_values, angles)
    inner_parts = jnp.moveaxis(
        inner_terms.reshape(2, quad_count, inner_rows // quad_count, 2 * probe_width), 1, 0
    )
    owned_parts = jnp.moveaxis(
        owned_terms.reshape(2, quad_count, owned_rows // quad_count, 2 * probe_width), 1, 0
    )
    both = jnp.concatenate([inner_parts, owned_parts], axis=2).astype(BF16)
    summed_both = lax.all_to_all(both, "quad", split_axis=0, concat_axis=0, tiled=True)
    summed_both = summed_both.astype(F32).sum(axis=0)
    inner_moments = summed_both[:, : inner_rows // quad_count]
    owned_moments = summed_both[:, inner_rows // quad_count :]
    return (inner_moments, owned_moments)


def solution(mesh):
    return jax.shard_map(
        on_device,
        mesh=mesh,
        in_specs=(
            P("quad", None, "area", None),
            P("area", None),
            P("area", None),
            P("area"),
            P(),
            P("area"),
        ),
        out_specs=(P(None, ("area", "quad"), None), P(None, ("area", "quad"), None)),
        check_vma=False,
    )
```

```python
import math

import jax
import jax.numpy as jnp
from jax import lax
from jax.sharding import PartitionSpec as P

ITERS = 4
F32 = jnp.float32
BF16 = jnp.bfloat16


def split_hi_lo(value):
    high = value.astype(BF16)
    low = (value - high.astype(F32)).astype(BF16)
    return high, low


def split_three(value):
    first = value.astype(BF16)
    rest = value - first.astype(F32)
    second = rest.astype(BF16)
    third = (rest - second.astype(F32)).astype(BF16)
    return first, second, third


def dot_split(spec, left_parts, right_parts):
    total = None
    for left in left_parts:
        for right in right_parts:
            term = jnp.einsum(spec, left, right, preferred_element_type=F32)
            total = term if total is None else total + term
    return total


def complex_block(values):
    width_half = values.shape[-1] // 2
    value_re = values[..., :width_half]
    value_im = values[..., width_half:]
    lower = jnp.concatenate([-value_im, value_re], axis=-1)
    return jnp.concatenate([values, lower], axis=-2)


def divide_rows(summed, shift_re, shift_im, diagonal_rows):
    width_half = summed.shape[-1] // 2
    real_den = shift_re[:, None] - diagonal_rows[None, :]
    imag_den = shift_im[:, None] * jnp.ones_like(diagonal_rows)[None, :]
    norm_den = real_den * real_den + imag_den * imag_den
    summed_re = summed[..., :width_half]
    summed_im = summed[..., width_half:]
    new_re = (summed_re * real_den[..., None] + summed_im * imag_den[..., None]) / norm_den[
        ..., None
    ]
    new_im = (summed_im * real_den[..., None] - summed_re * imag_den[..., None]) / norm_den[
        ..., None
    ]
    return jnp.concatenate([new_re, new_im], axis=-1)


def sent_and_summed(value, axis, dim):
    before, after = (value.shape[:dim], value.shape[dim + 1 :])
    parts = jnp.moveaxis(value.reshape(*before, lax.axis_size(axis), -1, *after), dim, 0)
    arrived = lax.all_to_all(parts, axis, split_axis=0, concat_axis=0, tiled=True)
    return arrived.sum(axis=0)


def weight_moments(values, angles):
    width_half = values.shape[-1] // 2
    value_re = values[..., :width_half]
    value_im = values[..., width_half:]
    results = []
    for power_index in (1, 2):
        cosine_now = jnp.cos(power_index * angles)[:, None, None]
        sine_now = jnp.sin(power_index * angles)[:, None, None]
        real_term = jnp.sum(cosine_now * value_re - sine_now * value_im, axis=0)
        imag_term = jnp.sum(cosine_now * value_im + sine_now * value_re, axis=0)
        results.append(jnp.concatenate([real_term, imag_term], axis=-1))
    return jnp.stack(results)


def on_device(inverses, coupling, probes, interface_diagonal, area_rows, live_counts):
    local_points = inverses.shape[0]
    area_count = lax.axis_size("area")
    quad_count = lax.axis_size("quad")
    area_index = lax.axis_index("area")
    shared_rows = coupling.shape[1]
    probe_width = probes.shape[1]
    owned_rows = interface_diagonal.shape[0]
    bucket = shared_rows // area_count
    live_mask = jnp.arange(shared_rows) < live_counts[0]
    coupling_live = jnp.where(live_mask[None, :], coupling, jnp.zeros_like(coupling))
    right = jnp.concatenate([probes, coupling_live], axis=1)
    applied = jnp.einsum("qrij,jc->qric", inverses, right, preferred_element_type=F32)
    projected = jnp.einsum(
        "ig,qric->qrgc", coupling_live, applied.astype(BF16), preferred_element_type=F32
    )
    probe_state = jnp.concatenate(
        [applied[:, 0, :, :probe_width], applied[:, 1, :, :probe_width]], axis=-1
    )
    state_map = jnp.concatenate(
        [applied[:, 0, :, probe_width:], applied[:, 1, :, probe_width:]], axis=-1
    )
    reply_start = jnp.concatenate(
        [projected[:, 0, :, :probe_width], projected[:, 1, :, :probe_width]], axis=-1
    )
    reply_map = jnp.concatenate(
        [projected[:, 0, :, probe_width:], projected[:, 1, :, probe_width:]], axis=-1
    )
    reply_parts = split_hi_lo(reply_map)
    block_offsets = (
        lax.dynamic_slice_in_dim(area_rows, area_index * bucket, bucket, 1)
        - area_index * owned_rows
    )
    flat_offsets = block_offsets.reshape(-1)
    selector = (flat_offsets[None, :] == jnp.arange(owned_rows)[:, None]).astype(BF16)
    selector = selector.reshape(owned_rows, area_count, bucket)
    angle_step = jnp.float32(2.0 * math.pi / (local_points * quad_count))
    point_ids = lax.axis_index("quad") * local_points + jnp.arange(local_points, dtype=jnp.int32)
    angles = (point_ids.astype(jnp.float32) + 0.5) * angle_step
    shift_re = jnp.cos(angles)
    shift_im = jnp.sin(angles)
    gathered_block = None
    interface_values = None
    for sweep_index in range(ITERS):
        if sweep_index == 0:
            replies = reply_start
        else:
            replies = reply_start + dot_split("qgh,qhc->qgc", reply_parts, (gathered_block,))
        parcels = jnp.moveaxis(
            replies.reshape(local_points, area_count, bucket, 2 * probe_width), 1, 0
        ).astype(BF16)
        arrived = lax.all_to_all(parcels, "area", split_axis=0, concat_axis=0, tiled=True)
        summed = jnp.einsum("rbs,bqsc->qrc", selector, arrived, preferred_element_type=F32)
        interface_values = divide_rows(summed, shift_re, shift_im, interface_diagonal)
        outgoing = jnp.einsum(
            "rbs,qrc->bqsc",
            selector,
            interface_values.astype(BF16),
            preferred_element_type=F32,
        ).astype(BF16)
        returned = lax.all_to_all(outgoing, "area", split_axis=0, concat_axis=0, tiled=True)
        gathered_rows = jnp.moveaxis(returned, 0, 1).reshape(
            local_points, shared_rows, 2 * probe_width
        )
        gathered_block = complex_block(gathered_rows)
    states = probe_state + jnp.einsum(
        "qih,qhc->qic", state_map.astype(BF16), gathered_block, preferred_element_type=F32
    )
    inner_rows = states.shape[1]
    inner_terms = weight_moments(states, angles)
    owned_terms = weight_moments(interface_values, angles)
    inner_parts = jnp.moveaxis(
        inner_terms.reshape(2, quad_count, inner_rows // quad_count, 2 * probe_width), 1, 0
    )
    owned_parts = jnp.moveaxis(
        owned_terms.reshape(2, quad_count, owned_rows // quad_count, 2 * probe_width), 1, 0
    )
    both = jnp.concatenate([inner_parts, owned_parts], axis=2).astype(BF16)
    summed_both = lax.all_to_all(both, "quad", split_axis=0, concat_axis=0, tiled=True)
    inner_moments = summed_both[:, :, : inner_rows // quad_count].astype(F32).sum(axis=0)
    owned_moments = summed_both[:, :, inner_rows // quad_count :].astype(F32).sum(axis=0)
    return (inner_moments, owned_moments)


def solution(mesh):
    return jax.shard_map(
        on_device,
        mesh=mesh,
        in_specs=(
            P("quad", None, "area", None),
            P("area", None),
            P("area", None),
            P("area"),
            P(),
            P("area"),
        ),
        out_specs=(P(None, ("area", "quad"), None), P(None, ("area", "quad"), None)),
        check_vma=False,
    )
```

```python
import math

import jax
import jax.numpy as jnp
from jax import lax
from jax.sharding import PartitionSpec as P

ITERS = 4
F32 = jnp.float32
BF16 = jnp.bfloat16


def dot_split(spec, left_parts, right_parts):
    total = None
    for left in left_parts:
        for right in right_parts:
            term = jnp.einsum(spec, left, right, preferred_element_type=F32)
            total = term if total is None else total + term
    return total


def complex_block(values):
    width_half = values.shape[-1] // 2
    value_re = values[..., :width_half]
    value_im = values[..., width_half:]
    lower = jnp.concatenate([-value_im, value_re], axis=-1)
    return jnp.concatenate([values, lower], axis=-2)


def divide_rows(summed, shift_re, shift_im, diagonal_rows):
    width_half = summed.shape[-1] // 2
    real_den = shift_re[:, None] - diagonal_rows[None, :]
    imag_den = shift_im[:, None] * jnp.ones_like(diagonal_rows)[None, :]
    norm_den = real_den * real_den + imag_den * imag_den
    summed_re = summed[..., :width_half]
    summed_im = summed[..., width_half:]
    new_re = (summed_re * real_den[..., None] + summed_im * imag_den[..., None]) / norm_den[
        ..., None
    ]
    new_im = (summed_im * real_den[..., None] - summed_re * imag_den[..., None]) / norm_den[
        ..., None
    ]
    return jnp.concatenate([new_re, new_im], axis=-1)


def sent_and_summed(value, axis, dim):
    before, after = (value.shape[:dim], value.shape[dim + 1 :])
    parts = jnp.moveaxis(value.reshape(*before, lax.axis_size(axis), -1, *after), dim, 0)
    arrived = lax.all_to_all(parts, axis, split_axis=0, concat_axis=0, tiled=True)
    return arrived.sum(axis=0)


def weight_moments(values, angles):
    width_half = values.shape[-1] // 2
    value_re = values[..., :width_half]
    value_im = values[..., width_half:]
    results = []
    for power_index in (1, 2):
        cosine_now = jnp.cos(power_index * angles)[:, None, None]
        sine_now = jnp.sin(power_index * angles)[:, None, None]
        real_term = jnp.sum(cosine_now * value_re - sine_now * value_im, axis=0)
        imag_term = jnp.sum(cosine_now * value_im + sine_now * value_re, axis=0)
        results.append(jnp.concatenate([real_term, imag_term], axis=-1))
    return jnp.stack(results)


def on_device(inverses, coupling, probes, interface_diagonal, area_rows, live_counts):
    local_points = inverses.shape[0]
    area_count = lax.axis_size("area")
    quad_count = lax.axis_size("quad")
    area_index = lax.axis_index("area")
    shared_rows = coupling.shape[1]
    probe_width = probes.shape[1]
    owned_rows = interface_diagonal.shape[0]
    bucket = shared_rows // area_count
    live_mask = jnp.arange(shared_rows) < live_counts[0]
    coupling_live = jnp.where(live_mask[None, :], coupling, jnp.zeros_like(coupling))
    right = jnp.concatenate([probes, coupling_live], axis=1)
    applied = jnp.einsum("qrij,jc->qric", inverses, right, preferred_element_type=F32)
    applied = applied.astype(BF16)
    projected = jnp.einsum("ig,qric->qrgc", coupling_live, applied, preferred_element_type=F32)
    probe_state = jnp.concatenate(
        [applied[:, 0, :, :probe_width], applied[:, 1, :, :probe_width]], axis=-1
    )
    state_map = jnp.concatenate(
        [applied[:, 0, :, probe_width:], applied[:, 1, :, probe_width:]], axis=-1
    )
    reply_start = jnp.concatenate(
        [projected[:, 0, :, :probe_width], projected[:, 1, :, :probe_width]], axis=-1
    )
    reply_map = jnp.concatenate(
        [projected[:, 0, :, probe_width:], projected[:, 1, :, probe_width:]], axis=-1
    )
    reply_parts = (reply_map.astype(BF16),)
    block_offsets = (
        lax.dynamic_slice_in_dim(area_rows, area_index * bucket, bucket, 1)
        - area_index * owned_rows
    )
    flat_offsets = block_offsets.reshape(-1)
    selector = (flat_offsets[None, :] == jnp.arange(owned_rows)[:, None]).astype(BF16)
    selector = selector.reshape(owned_rows, area_count, bucket)
    angle_step = jnp.float32(2.0 * math.pi / (local_points * quad_count))
    point_ids = lax.axis_index("quad") * local_points + jnp.arange(local_points, dtype=jnp.int32)
    angles = (point_ids.astype(jnp.float32) + 0.5) * angle_step
    shift_re = jnp.cos(angles)
    shift_im = jnp.sin(angles)
    gathered_block = None
    interface_values = None
    for sweep_index in range(ITERS):
        if sweep_index == 0:
            replies = reply_start
        else:
            replies = reply_start + dot_split("qgh,qhc->qgc", reply_parts, (gathered_block,))
        parcels = jnp.moveaxis(
            replies.reshape(local_points, area_count, bucket, 2 * probe_width), 1, 0
        ).astype(BF16)
        arrived = lax.all_to_all(parcels, "area", split_axis=0, concat_axis=0, tiled=True)
        summed = jnp.einsum("rbs,bqsc->qrc", selector, arrived, preferred_element_type=F32)
        interface_values = divide_rows(summed, shift_re, shift_im, interface_diagonal)
        outgoing = jnp.einsum(
            "rbs,qrc->bqsc",
            selector,
            interface_values.astype(BF16),
            preferred_element_type=F32,
        ).astype(BF16)
        returned = lax.all_to_all(outgoing, "area", split_axis=0, concat_axis=0, tiled=True)
        gathered_rows = jnp.moveaxis(returned, 0, 1).reshape(
            local_points, shared_rows, 2 * probe_width
        )
        gathered_block = complex_block(gathered_rows)
    states = probe_state.astype(F32) + jnp.einsum(
        "qih,qhc->qic", state_map, gathered_block, preferred_element_type=F32
    )
    inner_rows = states.shape[1]
    inner_terms = weight_moments(states, angles)
    owned_terms = weight_moments(interface_values, angles)
    inner_parts = jnp.moveaxis(
        inner_terms.reshape(2, quad_count, inner_rows // quad_count, 2 * probe_width), 1, 0
    )
    owned_parts = jnp.moveaxis(
        owned_terms.reshape(2, quad_count, owned_rows // quad_count, 2 * probe_width), 1, 0
    )
    both = jnp.concatenate([inner_parts, owned_parts], axis=2).astype(BF16)
    summed_both = lax.all_to_all(both, "quad", split_axis=0, concat_axis=0, tiled=True)
    inner_moments = summed_both[:, :, : inner_rows // quad_count].astype(F32).sum(axis=0)
    owned_moments = summed_both[:, :, inner_rows // quad_count :].astype(F32).sum(axis=0)
    return (inner_moments, owned_moments)


def solution(mesh):
    return jax.shard_map(
        on_device,
        mesh=mesh,
        in_specs=(
            P("quad", None, "area", None),
            P("area", None),
            P("area", None),
            P("area"),
            P(),
            P("area"),
        ),
        out_specs=(P(None, ("area", "quad"), None), P(None, ("area", "quad"), None)),
        check_vma=False,
    )
```

```python
import math

import jax
import jax.numpy as jnp
from jax import lax
from jax.sharding import PartitionSpec as P

ITERS = 4
F32 = jnp.float32
BF16 = jnp.bfloat16


def dot_split(spec, left_parts, right_parts):
    total = None
    for left in left_parts:
        for right in right_parts:
            term = jnp.einsum(spec, left, right, preferred_element_type=F32)
            total = term if total is None else total + term
    return total


def complex_block(values):
    width_half = values.shape[-1] // 2
    value_re = values[..., :width_half]
    value_im = values[..., width_half:]
    lower = jnp.concatenate([-value_im, value_re], axis=-1)
    return jnp.concatenate([values, lower], axis=-2)


def divide_rows(summed, shift_re, shift_im, diagonal_rows):
    width_half = summed.shape[-1] // 2
    real_den = shift_re[:, None] - diagonal_rows[None, :]
    imag_den = shift_im[:, None] * jnp.ones_like(diagonal_rows)[None, :]
    norm_den = real_den * real_den + imag_den * imag_den
    summed_re = summed[..., :width_half]
    summed_im = summed[..., width_half:]
    new_re = (summed_re * real_den[..., None] + summed_im * imag_den[..., None]) / norm_den[
        ..., None
    ]
    new_im = (summed_im * real_den[..., None] - summed_re * imag_den[..., None]) / norm_den[
        ..., None
    ]
    return jnp.concatenate([new_re, new_im], axis=-1)


def sent_and_summed(value, axis, dim):
    before, after = (value.shape[:dim], value.shape[dim + 1 :])
    parts = jnp.moveaxis(value.reshape(*before, lax.axis_size(axis), -1, *after), dim, 0)
    arrived = lax.all_to_all(parts, axis, split_axis=0, concat_axis=0, tiled=True)
    return arrived.sum(axis=0)


def weight_moments(values, angles):
    width_half = values.shape[-1] // 2
    value_re = values[..., :width_half]
    value_im = values[..., width_half:]
    results = []
    for power_index in (1, 2):
        cosine_now = jnp.cos(power_index * angles)[:, None, None]
        sine_now = jnp.sin(power_index * angles)[:, None, None]
        real_term = jnp.sum(cosine_now * value_re - sine_now * value_im, axis=0)
        imag_term = jnp.sum(cosine_now * value_im + sine_now * value_re, axis=0)
        results.append(jnp.concatenate([real_term, imag_term], axis=-1))
    return jnp.stack(results)


def on_device(inverses, coupling, probes, interface_diagonal, area_rows, live_counts):
    local_points = inverses.shape[0]
    area_count = lax.axis_size("area")
    quad_count = lax.axis_size("quad")
    area_index = lax.axis_index("area")
    shared_rows = coupling.shape[1]
    probe_width = probes.shape[1]
    owned_rows = interface_diagonal.shape[0]
    bucket = shared_rows // area_count
    live_mask = jnp.arange(shared_rows) < live_counts[0]
    coupling_live = jnp.where(live_mask[None, :], coupling, jnp.zeros_like(coupling))
    right = jnp.concatenate([probes, coupling_live], axis=1)
    applied = jnp.einsum("qrij,jc->qric", inverses, right, preferred_element_type=F32)
    applied = applied.astype(BF16)
    projected = jnp.einsum("ig,qric->qrgc", coupling_live, applied, preferred_element_type=F32)
    probe_state = jnp.concatenate(
        [applied[:, 0, :, :probe_width], applied[:, 1, :, :probe_width]], axis=-1
    )
    reply_start = jnp.concatenate(
        [projected[:, 0, :, :probe_width], projected[:, 1, :, :probe_width]], axis=-1
    )
    reply_map = jnp.concatenate(
        [projected[:, 0, :, probe_width:], projected[:, 1, :, probe_width:]], axis=-1
    )
    reply_parts = (reply_map.astype(BF16),)
    block_offsets = (
        lax.dynamic_slice_in_dim(area_rows, area_index * bucket, bucket, 1)
        - area_index * owned_rows
    )
    flat_offsets = block_offsets.reshape(-1)
    selector = (flat_offsets[None, :] == jnp.arange(owned_rows)[:, None]).astype(BF16)
    selector = selector.reshape(owned_rows, area_count, bucket)
    angle_step = jnp.float32(2.0 * math.pi / (local_points * quad_count))
    point_ids = lax.axis_index("quad") * local_points + jnp.arange(local_points, dtype=jnp.int32)
    angles = (point_ids.astype(jnp.float32) + 0.5) * angle_step
    shift_re = jnp.cos(angles)
    shift_im = jnp.sin(angles)
    gathered_block = None
    interface_values = None
    for sweep_index in range(ITERS):
        if sweep_index == 0:
            replies = reply_start
        else:
            replies = reply_start + dot_split("qgh,qhc->qgc", reply_parts, (gathered_block,))
        parcels = jnp.moveaxis(
            replies.reshape(local_points, area_count, bucket, 2 * probe_width), 1, 0
        ).astype(BF16)
        arrived = lax.all_to_all(parcels, "area", split_axis=0, concat_axis=0, tiled=True)
        summed = jnp.einsum("rbs,bqsc->qrc", selector, arrived, preferred_element_type=F32)
        interface_values = divide_rows(summed, shift_re, shift_im, interface_diagonal)
        outgoing = jnp.einsum(
            "rbs,qrc->bqsc",
            selector,
            interface_values.astype(BF16),
            preferred_element_type=F32,
        ).astype(BF16)
        returned = lax.all_to_all(outgoing, "area", split_axis=0, concat_axis=0, tiled=True)
        gathered_rows = jnp.moveaxis(returned, 0, 1).reshape(
            local_points, shared_rows, 2 * probe_width
        )
        gathered_block = complex_block(gathered_rows)
    part_block = gathered_block.reshape(local_points, 2, shared_rows, 2 * probe_width)
    states = probe_state.astype(F32) + jnp.einsum(
        "qris,qrsc->qic", applied[..., probe_width:], part_block, preferred_element_type=F32
    )
    inner_rows = states.shape[1]
    inner_terms = weight_moments(states, angles)
    owned_terms = weight_moments(interface_values, angles)
    inner_parts = jnp.moveaxis(
        inner_terms.reshape(2, quad_count, inner_rows // quad_count, 2 * probe_width), 1, 0
    )
    owned_parts = jnp.moveaxis(
        owned_terms.reshape(2, quad_count, owned_rows // quad_count, 2 * probe_width), 1, 0
    )
    both = jnp.concatenate([inner_parts, owned_parts], axis=2).astype(BF16)
    summed_both = lax.all_to_all(both, "quad", split_axis=0, concat_axis=0, tiled=True)
    inner_moments = summed_both[:, :, : inner_rows // quad_count].astype(F32).sum(axis=0)
    owned_moments = summed_both[:, :, inner_rows // quad_count :].astype(F32).sum(axis=0)
    return (inner_moments, owned_moments)


def solution(mesh):
    return jax.shard_map(
        on_device,
        mesh=mesh,
        in_specs=(
            P("quad", None, "area", None),
            P("area", None),
            P("area", None),
            P("area"),
            P(),
            P("area"),
        ),
        out_specs=(P(None, ("area", "quad"), None), P(None, ("area", "quad"), None)),
        check_vma=False,
    )
```

```python
import math

import jax
import jax.numpy as jnp
from jax import lax
from jax.sharding import PartitionSpec as P

ITERS = 4
F32 = jnp.float32
BF16 = jnp.bfloat16


def dot_split(spec, left_parts, right_parts):
    total = None
    for left in left_parts:
        for right in right_parts:
            term = jnp.einsum(spec, left, right, preferred_element_type=F32)
            total = term if total is None else total + term
    return total


def complex_block(values):
    width_half = values.shape[-1] // 2
    value_re = values[..., :width_half]
    value_im = values[..., width_half:]
    lower = jnp.concatenate([-value_im, value_re], axis=-1)
    return jnp.concatenate([values, lower], axis=-2)


def divide_rows(summed, shift_re, shift_im, diagonal_rows):
    width_half = summed.shape[-1] // 2
    real_den = shift_re[:, None] - diagonal_rows[None, :]
    imag_den = shift_im[:, None] * jnp.ones_like(diagonal_rows)[None, :]
    norm_den = real_den * real_den + imag_den * imag_den
    summed_re = summed[..., :width_half]
    summed_im = summed[..., width_half:]
    new_re = (summed_re * real_den[..., None] + summed_im * imag_den[..., None]) / norm_den[
        ..., None
    ]
    new_im = (summed_im * real_den[..., None] - summed_re * imag_den[..., None]) / norm_den[
        ..., None
    ]
    return jnp.concatenate([new_re, new_im], axis=-1)


def sent_and_summed(value, axis, dim):
    before, after = (value.shape[:dim], value.shape[dim + 1 :])
    parts = jnp.moveaxis(value.reshape(*before, lax.axis_size(axis), -1, *after), dim, 0)
    arrived = lax.all_to_all(parts, axis, split_axis=0, concat_axis=0, tiled=True)
    return arrived.sum(axis=0)


def rotate(values, angles, power):
    width_half = values.shape[-1] // 2
    value_re = values[..., :width_half]
    value_im = values[..., width_half:]
    cosine_now = jnp.cos(power * angles)[:, None, None]
    sine_now = jnp.sin(power * angles)[:, None, None]
    return jnp.concatenate(
        [cosine_now * value_re - sine_now * value_im, cosine_now * value_im + sine_now * value_re],
        axis=-1,
    )


def weight_moments(values, angles):
    width_half = values.shape[-1] // 2
    value_re = values[..., :width_half]
    value_im = values[..., width_half:]
    results = []
    for power_index in (1, 2):
        cosine_now = jnp.cos(power_index * angles)[:, None, None]
        sine_now = jnp.sin(power_index * angles)[:, None, None]
        real_term = jnp.sum(cosine_now * value_re - sine_now * value_im, axis=0)
        imag_term = jnp.sum(cosine_now * value_im + sine_now * value_re, axis=0)
        results.append(jnp.concatenate([real_term, imag_term], axis=-1))
    return jnp.stack(results)


def on_device(inverses, coupling, probes, interface_diagonal, area_rows, live_counts):
    local_points = inverses.shape[0]
    area_count = lax.axis_size("area")
    quad_count = lax.axis_size("quad")
    area_index = lax.axis_index("area")
    shared_rows = coupling.shape[1]
    probe_width = probes.shape[1]
    owned_rows = interface_diagonal.shape[0]
    bucket = shared_rows // area_count
    live_mask = jnp.arange(shared_rows) < live_counts[0]
    coupling_live = jnp.where(live_mask[None, :], coupling, jnp.zeros_like(coupling))
    right = jnp.concatenate([probes, coupling_live], axis=1)
    applied = jnp.einsum("qrij,jc->qric", inverses, right, preferred_element_type=F32)
    applied = applied.astype(BF16)
    projected = jnp.einsum("ig,qric->qrgc", coupling_live, applied, preferred_element_type=F32)
    probe_state = jnp.concatenate(
        [applied[:, 0, :, :probe_width], applied[:, 1, :, :probe_width]], axis=-1
    )
    reply_start = jnp.concatenate(
        [projected[:, 0, :, :probe_width], projected[:, 1, :, :probe_width]], axis=-1
    )
    reply_map = jnp.concatenate(
        [projected[:, 0, :, probe_width:], projected[:, 1, :, probe_width:]], axis=-1
    )
    reply_parts = (reply_map.astype(BF16),)
    block_offsets = (
        lax.dynamic_slice_in_dim(area_rows, area_index * bucket, bucket, 1)
        - area_index * owned_rows
    )
    flat_offsets = block_offsets.reshape(-1)
    selector = (flat_offsets[None, :] == jnp.arange(owned_rows)[:, None]).astype(BF16)
    selector = selector.reshape(owned_rows, area_count, bucket)
    angle_step = jnp.float32(2.0 * math.pi / (local_points * quad_count))
    point_ids = lax.axis_index("quad") * local_points + jnp.arange(local_points, dtype=jnp.int32)
    angles = (point_ids.astype(jnp.float32) + 0.5) * angle_step
    shift_re = jnp.cos(angles)
    shift_im = jnp.sin(angles)
    gathered_block = None
    interface_values = None
    for sweep_index in range(ITERS):
        if sweep_index == 0:
            replies = reply_start
        else:
            replies = reply_start + dot_split("qgh,qhc->qgc", reply_parts, (gathered_block,))
        parcels = jnp.moveaxis(
            replies.reshape(local_points, area_count, bucket, 2 * probe_width), 1, 0
        ).astype(BF16)
        arrived = lax.all_to_all(parcels, "area", split_axis=0, concat_axis=0, tiled=True)
        summed = jnp.einsum("rbs,bqsc->qrc", selector, arrived, preferred_element_type=F32)
        interface_values = divide_rows(summed, shift_re, shift_im, interface_diagonal)
        outgoing = jnp.einsum(
            "rbs,qrc->bqsc",
            selector,
            interface_values.astype(BF16),
            preferred_element_type=F32,
        ).astype(BF16)
        returned = lax.all_to_all(outgoing, "area", split_axis=0, concat_axis=0, tiled=True)
        gathered_rows = jnp.moveaxis(returned, 0, 1).reshape(
            local_points, shared_rows, 2 * probe_width
        )
        gathered_block = complex_block(gathered_rows)
    inner_rows = probe_state.shape[1]
    gathered_float = gathered_rows.astype(F32)
    weighted_block = jnp.stack(
        [complex_block(rotate(gathered_float, angles, power)) for power in (1, 2)]
    ).astype(BF16)
    weighted_block = weighted_block.reshape(2, local_points, 2, shared_rows, 2 * probe_width)
    inner_terms = weight_moments(probe_state.astype(F32), angles) + jnp.einsum(
        "qris,mqrsc->mic",
        applied[..., probe_width:],
        weighted_block,
        preferred_element_type=F32,
    )
    owned_terms = weight_moments(interface_values, angles)
    inner_parts = jnp.moveaxis(
        inner_terms.reshape(2, quad_count, inner_rows // quad_count, 2 * probe_width), 1, 0
    )
    owned_parts = jnp.moveaxis(
        owned_terms.reshape(2, quad_count, owned_rows // quad_count, 2 * probe_width), 1, 0
    )
    both = jnp.concatenate([inner_parts, owned_parts], axis=2).astype(BF16)
    summed_both = lax.all_to_all(both, "quad", split_axis=0, concat_axis=0, tiled=True)
    inner_moments = summed_both[:, :, : inner_rows // quad_count].astype(F32).sum(axis=0)
    owned_moments = summed_both[:, :, inner_rows // quad_count :].astype(F32).sum(axis=0)
    return (inner_moments, owned_moments)


def solution(mesh):
    return jax.shard_map(
        on_device,
        mesh=mesh,
        in_specs=(
            P("quad", None, "area", None),
            P("area", None),
            P("area", None),
            P("area"),
            P(),
            P("area"),
        ),
        out_specs=(P(None, ("area", "quad"), None), P(None, ("area", "quad"), None)),
        check_vma=False,
    )
```

```python
import math

import jax
import jax.numpy as jnp
from jax import lax
from jax.sharding import PartitionSpec as P

ITERS = 4
F32 = jnp.float32
BF16 = jnp.bfloat16


def dot_split(spec, left_parts, right_parts):
    total = None
    for left in left_parts:
        for right in right_parts:
            term = jnp.einsum(spec, left, right, preferred_element_type=F32)
            total = term if total is None else total + term
    return total


def complex_block(values):
    width_half = values.shape[-1] // 2
    value_re = values[..., :width_half]
    value_im = values[..., width_half:]
    lower = jnp.concatenate([-value_im, value_re], axis=-1)
    return jnp.concatenate([values, lower], axis=-2)


def divide_rows(summed, shift_re, shift_im, diagonal_rows):
    width_half = summed.shape[-1] // 2
    real_den = shift_re[:, None] - diagonal_rows[None, :]
    imag_den = shift_im[:, None] * jnp.ones_like(diagonal_rows)[None, :]
    norm_den = real_den * real_den + imag_den * imag_den
    summed_re = summed[..., :width_half]
    summed_im = summed[..., width_half:]
    new_re = (summed_re * real_den[..., None] + summed_im * imag_den[..., None]) / norm_den[
        ..., None
    ]
    new_im = (summed_im * real_den[..., None] - summed_re * imag_den[..., None]) / norm_den[
        ..., None
    ]
    return jnp.concatenate([new_re, new_im], axis=-1)


def sent_and_summed(value, axis, dim):
    before, after = (value.shape[:dim], value.shape[dim + 1 :])
    parts = jnp.moveaxis(value.reshape(*before, lax.axis_size(axis), -1, *after), dim, 0)
    arrived = lax.all_to_all(parts, axis, split_axis=0, concat_axis=0, tiled=True)
    return arrived.sum(axis=0)


def weight_moments(values, angles):
    width_half = values.shape[-1] // 2
    value_re = values[..., :width_half]
    value_im = values[..., width_half:]
    results = []
    for power_index in (1, 2):
        cosine_now = jnp.cos(power_index * angles)[:, None, None]
        sine_now = jnp.sin(power_index * angles)[:, None, None]
        real_term = jnp.sum(cosine_now * value_re - sine_now * value_im, axis=0)
        imag_term = jnp.sum(cosine_now * value_im + sine_now * value_re, axis=0)
        results.append(jnp.concatenate([real_term, imag_term], axis=-1))
    return jnp.stack(results)


def on_device(inverses, coupling, probes, interface_diagonal, area_rows, live_counts):
    local_points = inverses.shape[0]
    area_count = lax.axis_size("area")
    quad_count = lax.axis_size("quad")
    area_index = lax.axis_index("area")
    shared_rows = coupling.shape[1]
    probe_width = probes.shape[1]
    owned_rows = interface_diagonal.shape[0]
    bucket = shared_rows // area_count
    live_mask = jnp.arange(shared_rows) < live_counts[0]
    coupling_live = jnp.where(live_mask[None, :], coupling, jnp.zeros_like(coupling))
    right = jnp.concatenate([probes, coupling_live], axis=1)
    applied = jnp.einsum("qrij,jc->qric", inverses, right, preferred_element_type=F32)
    applied = applied.astype(BF16)
    projected_probe = jnp.einsum(
        "ig,qric->qrgc", coupling_live, applied[..., :probe_width], preferred_element_type=F32
    )
    projected_map = jnp.einsum(
        "ig,qric->qrgc", coupling_live, applied[..., probe_width:], preferred_element_type=F32
    )
    probe_state = jnp.concatenate(
        [applied[:, 0, :, :probe_width], applied[:, 1, :, :probe_width]], axis=-1
    )
    reply_start = jnp.concatenate([projected_probe[:, 0], projected_probe[:, 1]], axis=-1)
    reply_map = jnp.concatenate([projected_map[:, 0], projected_map[:, 1]], axis=-1)
    reply_parts = (reply_map.astype(BF16),)
    block_offsets = (
        lax.dynamic_slice_in_dim(area_rows, area_index * bucket, bucket, 1)
        - area_index * owned_rows
    )
    flat_offsets = block_offsets.reshape(-1)
    selector = (flat_offsets[None, :] == jnp.arange(owned_rows)[:, None]).astype(BF16)
    selector = selector.reshape(owned_rows, area_count, bucket)
    angle_step = jnp.float32(2.0 * math.pi / (local_points * quad_count))
    point_ids = lax.axis_index("quad") * local_points + jnp.arange(local_points, dtype=jnp.int32)
    angles = (point_ids.astype(jnp.float32) + 0.5) * angle_step
    shift_re = jnp.cos(angles)
    shift_im = jnp.sin(angles)
    gathered_block = None
    interface_values = None
    for sweep_index in range(ITERS):
        if sweep_index == 0:
            replies = reply_start
        else:
            replies = reply_start + dot_split("qgh,qhc->qgc", reply_parts, (gathered_block,))
        parcels = jnp.moveaxis(
            replies.reshape(local_points, area_count, bucket, 2 * probe_width), 1, 0
        ).astype(BF16)
        arrived = lax.all_to_all(parcels, "area", split_axis=0, concat_axis=0, tiled=True)
        summed = jnp.einsum("rbs,bqsc->qrc", selector, arrived, preferred_element_type=F32)
        interface_values = divide_rows(summed, shift_re, shift_im, interface_diagonal)
        outgoing = jnp.einsum(
            "rbs,qrc->bqsc",
            selector,
            interface_values.astype(BF16),
            preferred_element_type=F32,
        ).astype(BF16)
        returned = lax.all_to_all(outgoing, "area", split_axis=0, concat_axis=0, tiled=True)
        gathered_rows = jnp.moveaxis(returned, 0, 1).reshape(
            local_points, shared_rows, 2 * probe_width
        )
        gathered_block = complex_block(gathered_rows)
    part_block = gathered_block.reshape(local_points, 2, shared_rows, 2 * probe_width)
    states = probe_state.astype(F32) + jnp.einsum(
        "qris,qrsc->qic", applied[..., probe_width:], part_block, preferred_element_type=F32
    )
    inner_rows = states.shape[1]
    inner_terms = weight_moments(states, angles)
    owned_terms = weight_moments(interface_values, angles)
    inner_parts = jnp.moveaxis(
        inner_terms.reshape(2, quad_count, inner_rows // quad_count, 2 * probe_width), 1, 0
    )
    owned_parts = jnp.moveaxis(
        owned_terms.reshape(2, quad_count, owned_rows // quad_count, 2 * probe_width), 1, 0
    )
    both = jnp.concatenate([inner_parts, owned_parts], axis=2).astype(BF16)
    summed_both = lax.all_to_all(both, "quad", split_axis=0, concat_axis=0, tiled=True)
    inner_moments = summed_both[:, :, : inner_rows // quad_count].astype(F32).sum(axis=0)
    owned_moments = summed_both[:, :, inner_rows // quad_count :].astype(F32).sum(axis=0)
    return (inner_moments, owned_moments)


def solution(mesh):
    return jax.shard_map(
        on_device,
        mesh=mesh,
        in_specs=(
            P("quad", None, "area", None),
            P("area", None),
            P("area", None),
            P("area"),
            P(),
            P("area"),
        ),
        out_specs=(P(None, ("area", "quad"), None), P(None, ("area", "quad"), None)),
        check_vma=False,
    )
```

```python
import math

import jax
import jax.numpy as jnp
from jax import lax
from jax.sharding import PartitionSpec as P

ITERS = 4
F32 = jnp.float32
BF16 = jnp.bfloat16


def dot_split(spec, left_parts, right_parts):
    total = None
    for left in left_parts:
        for right in right_parts:
            term = jnp.einsum(spec, left, right, preferred_element_type=F32)
            total = term if total is None else total + term
    return total


def complex_block(values):
    width_half = values.shape[-1] // 2
    value_re = values[..., :width_half]
    value_im = values[..., width_half:]
    lower = jnp.concatenate([-value_im, value_re], axis=-1)
    return jnp.concatenate([values, lower], axis=-2)


def divide_rows(summed, shift_re, shift_im, diagonal_rows):
    width_half = summed.shape[-1] // 2
    real_den = shift_re[:, None] - diagonal_rows[None, :]
    imag_den = shift_im[:, None] * jnp.ones_like(diagonal_rows)[None, :]
    norm_den = real_den * real_den + imag_den * imag_den
    summed_re = summed[..., :width_half]
    summed_im = summed[..., width_half:]
    new_re = (summed_re * real_den[..., None] + summed_im * imag_den[..., None]) / norm_den[
        ..., None
    ]
    new_im = (summed_im * real_den[..., None] - summed_re * imag_den[..., None]) / norm_den[
        ..., None
    ]
    return jnp.concatenate([new_re, new_im], axis=-1)


def sent_and_summed(value, axis, dim):
    before, after = (value.shape[:dim], value.shape[dim + 1 :])
    parts = jnp.moveaxis(value.reshape(*before, lax.axis_size(axis), -1, *after), dim, 0)
    arrived = lax.all_to_all(parts, axis, split_axis=0, concat_axis=0, tiled=True)
    return arrived.sum(axis=0)


def weight_moments(values, angles):
    width_half = values.shape[-1] // 2
    value_re = values[..., :width_half]
    value_im = values[..., width_half:]
    results = []
    for power_index in (1, 2):
        cosine_now = jnp.cos(power_index * angles)[:, None, None]
        sine_now = jnp.sin(power_index * angles)[:, None, None]
        real_term = jnp.sum(cosine_now * value_re - sine_now * value_im, axis=0)
        imag_term = jnp.sum(cosine_now * value_im + sine_now * value_re, axis=0)
        results.append(jnp.concatenate([real_term, imag_term], axis=-1))
    return jnp.stack(results)


def on_device(inverses, coupling, probes, interface_diagonal, area_rows, live_counts):
    local_points = inverses.shape[0]
    area_count = lax.axis_size("area")
    quad_count = lax.axis_size("quad")
    area_index = lax.axis_index("area")
    shared_rows = coupling.shape[1]
    probe_width = probes.shape[1]
    owned_rows = interface_diagonal.shape[0]
    bucket = shared_rows // area_count
    live_mask = jnp.arange(shared_rows) < live_counts[0]
    coupling_live = jnp.where(live_mask[None, :], coupling, jnp.zeros_like(coupling))
    applied_probe = jnp.einsum(
        "qrij,jc->qric", inverses, probes, preferred_element_type=F32
    ).astype(BF16)
    applied_map = jnp.einsum(
        "qrij,jc->qric", inverses, coupling_live, preferred_element_type=F32
    ).astype(BF16)
    projected_probe = jnp.einsum(
        "ig,qric->qrgc", coupling_live, applied_probe, preferred_element_type=F32
    )
    projected_map = jnp.einsum(
        "ig,qric->qrgc", coupling_live, applied_map, preferred_element_type=F32
    )
    probe_state = jnp.concatenate([applied_probe[:, 0], applied_probe[:, 1]], axis=-1)
    reply_start = jnp.concatenate([projected_probe[:, 0], projected_probe[:, 1]], axis=-1)
    reply_map = jnp.concatenate([projected_map[:, 0], projected_map[:, 1]], axis=-1)
    reply_parts = (reply_map.astype(BF16),)
    block_offsets = (
        lax.dynamic_slice_in_dim(area_rows, area_index * bucket, bucket, 1)
        - area_index * owned_rows
    )
    flat_offsets = block_offsets.reshape(-1)
    selector = (flat_offsets[None, :] == jnp.arange(owned_rows)[:, None]).astype(BF16)
    selector = selector.reshape(owned_rows, area_count, bucket)
    angle_step = jnp.float32(2.0 * math.pi / (local_points * quad_count))
    point_ids = lax.axis_index("quad") * local_points + jnp.arange(local_points, dtype=jnp.int32)
    angles = (point_ids.astype(jnp.float32) + 0.5) * angle_step
    shift_re = jnp.cos(angles)
    shift_im = jnp.sin(angles)
    gathered_block = None
    interface_values = None
    for sweep_index in range(ITERS):
        if sweep_index == 0:
            replies = reply_start
        else:
            replies = reply_start + dot_split("qgh,qhc->qgc", reply_parts, (gathered_block,))
        parcels = jnp.moveaxis(
            replies.reshape(local_points, area_count, bucket, 2 * probe_width), 1, 0
        ).astype(BF16)
        arrived = lax.all_to_all(parcels, "area", split_axis=0, concat_axis=0, tiled=True)
        summed = jnp.einsum("rbs,bqsc->qrc", selector, arrived, preferred_element_type=F32)
        interface_values = divide_rows(summed, shift_re, shift_im, interface_diagonal)
        outgoing = jnp.einsum(
            "rbs,qrc->bqsc",
            selector,
            interface_values.astype(BF16),
            preferred_element_type=F32,
        ).astype(BF16)
        returned = lax.all_to_all(outgoing, "area", split_axis=0, concat_axis=0, tiled=True)
        gathered_rows = jnp.moveaxis(returned, 0, 1).reshape(
            local_points, shared_rows, 2 * probe_width
        )
        gathered_block = complex_block(gathered_rows)
    part_block = gathered_block.reshape(local_points, 2, shared_rows, 2 * probe_width)
    states = probe_state.astype(F32) + jnp.einsum(
        "qris,qrsc->qic", applied_map, part_block, preferred_element_type=F32
    )
    inner_rows = states.shape[1]
    inner_terms = weight_moments(states, angles)
    owned_terms = weight_moments(interface_values, angles)
    inner_parts = jnp.moveaxis(
        inner_terms.reshape(2, quad_count, inner_rows // quad_count, 2 * probe_width), 1, 0
    )
    owned_parts = jnp.moveaxis(
        owned_terms.reshape(2, quad_count, owned_rows // quad_count, 2 * probe_width), 1, 0
    )
    both = jnp.concatenate([inner_parts, owned_parts], axis=2).astype(BF16)
    summed_both = lax.all_to_all(both, "quad", split_axis=0, concat_axis=0, tiled=True)
    inner_moments = summed_both[:, :, : inner_rows // quad_count].astype(F32).sum(axis=0)
    owned_moments = summed_both[:, :, inner_rows // quad_count :].astype(F32).sum(axis=0)
    return (inner_moments, owned_moments)


def solution(mesh):
    return jax.shard_map(
        on_device,
        mesh=mesh,
        in_specs=(
            P("quad", None, "area", None),
            P("area", None),
            P("area", None),
            P("area"),
            P(),
            P("area"),
        ),
        out_specs=(P(None, ("area", "quad"), None), P(None, ("area", "quad"), None)),
        check_vma=False,
    )
```

```python
import math

import jax
import jax.numpy as jnp
from jax import lax
from jax.sharding import PartitionSpec as P

ITERS = 4
F32 = jnp.float32
BF16 = jnp.bfloat16


def dot_split(spec, left_parts, right_parts):
    total = None
    for left in left_parts:
        for right in right_parts:
            term = jnp.einsum(spec, left, right, preferred_element_type=F32)
            total = term if total is None else total + term
    return total


def complex_block(values):
    width_half = values.shape[-1] // 2
    value_re = values[..., :width_half]
    value_im = values[..., width_half:]
    lower = jnp.concatenate([-value_im, value_re], axis=-1)
    return jnp.concatenate([values, lower], axis=-2)


def divide_rows(summed, shift_re, shift_im, diagonal_rows):
    width_half = summed.shape[-1] // 2
    real_den = shift_re[:, None] - diagonal_rows[None, :]
    imag_den = shift_im[:, None] * jnp.ones_like(diagonal_rows)[None, :]
    norm_den = real_den * real_den + imag_den * imag_den
    summed_re = summed[..., :width_half]
    summed_im = summed[..., width_half:]
    new_re = (summed_re * real_den[..., None] + summed_im * imag_den[..., None]) / norm_den[
        ..., None
    ]
    new_im = (summed_im * real_den[..., None] - summed_re * imag_den[..., None]) / norm_den[
        ..., None
    ]
    return jnp.concatenate([new_re, new_im], axis=-1)


def sent_and_summed(value, axis, dim):
    before, after = (value.shape[:dim], value.shape[dim + 1 :])
    parts = jnp.moveaxis(value.reshape(*before, lax.axis_size(axis), -1, *after), dim, 0)
    arrived = lax.all_to_all(parts, axis, split_axis=0, concat_axis=0, tiled=True)
    return arrived.sum(axis=0)


def weight_moments(values, angles):
    width_half = values.shape[-1] // 2
    value_re = values[..., :width_half]
    value_im = values[..., width_half:]
    results = []
    for power_index in (1, 2):
        cosine_now = jnp.cos(power_index * angles)[:, None, None]
        sine_now = jnp.sin(power_index * angles)[:, None, None]
        real_term = jnp.sum(cosine_now * value_re - sine_now * value_im, axis=0)
        imag_term = jnp.sum(cosine_now * value_im + sine_now * value_re, axis=0)
        results.append(jnp.concatenate([real_term, imag_term], axis=-1))
    return jnp.stack(results)


def on_device(inverses, coupling, probes, interface_diagonal, area_rows, live_counts):
    local_points = inverses.shape[0]
    area_count = lax.axis_size("area")
    quad_count = lax.axis_size("quad")
    area_index = lax.axis_index("area")
    shared_rows = coupling.shape[1]
    probe_width = probes.shape[1]
    owned_rows = interface_diagonal.shape[0]
    bucket = shared_rows // area_count
    live_mask = jnp.arange(shared_rows) < live_counts[0]
    coupling_live = jnp.where(live_mask[None, :], coupling, jnp.zeros_like(coupling))
    right = jnp.concatenate([probes, coupling_live], axis=1)
    applied = jnp.einsum("qrij,jc->qric", inverses, right, preferred_element_type=F32)
    applied = applied.astype(BF16)
    projected_probe = jnp.einsum(
        "ig,qric->qrgc", coupling_live, applied[..., :probe_width], preferred_element_type=F32
    )
    projected_map = jnp.einsum(
        "ig,qric->qrgc", coupling_live, applied[..., probe_width:], preferred_element_type=F32
    )
    probe_state = jnp.concatenate(
        [applied[:, 0, :, :probe_width], applied[:, 1, :, :probe_width]], axis=-1
    )
    reply_start = jnp.concatenate([projected_probe[:, 0], projected_probe[:, 1]], axis=-1)
    reply_map = jnp.concatenate([projected_map[:, 0], projected_map[:, 1]], axis=-1)
    reply_parts = (reply_map.astype(BF16),)
    block_offsets = (
        lax.dynamic_slice_in_dim(area_rows, area_index * bucket, bucket, 1)
        - area_index * owned_rows
    )
    flat_offsets = block_offsets.reshape(-1)
    selector = (flat_offsets[None, :] == jnp.arange(owned_rows)[:, None]).astype(BF16)
    selector = selector.reshape(owned_rows, area_count, bucket)
    angle_step = jnp.float32(2.0 * math.pi / (local_points * quad_count))
    point_ids = lax.axis_index("quad") * local_points + jnp.arange(local_points, dtype=jnp.int32)
    angles = (point_ids.astype(jnp.float32) + 0.5) * angle_step
    shift_re = jnp.cos(angles)
    shift_im = jnp.sin(angles)
    probe_terms = weight_moments(probe_state.astype(F32), angles)
    gathered_block = None
    interface_values = None
    for sweep_index in range(ITERS):
        if sweep_index == 0:
            replies = reply_start
        else:
            replies = reply_start + dot_split("qgh,qhc->qgc", reply_parts, (gathered_block,))
        parcels = jnp.moveaxis(
            replies.reshape(local_points, area_count, bucket, 2 * probe_width), 1, 0
        ).astype(BF16)
        arrived = lax.all_to_all(parcels, "area", split_axis=0, concat_axis=0, tiled=True)
        summed = jnp.einsum("rbs,bqsc->qrc", selector, arrived, preferred_element_type=F32)
        interface_values = divide_rows(summed, shift_re, shift_im, interface_diagonal)
        outgoing = jnp.einsum(
            "rbs,qrc->bqsc",
            selector,
            interface_values.astype(BF16),
            preferred_element_type=F32,
        ).astype(BF16)
        returned = lax.all_to_all(outgoing, "area", split_axis=0, concat_axis=0, tiled=True)
        gathered_rows = jnp.moveaxis(returned, 0, 1).reshape(
            local_points, shared_rows, 2 * probe_width
        )
        gathered_block = complex_block(gathered_rows)
    part_block = gathered_block.reshape(local_points, 2, shared_rows, 2 * probe_width)
    map_states = jnp.einsum(
        "qris,qrsc->qic", applied[..., probe_width:], part_block, preferred_element_type=F32
    )
    inner_rows = map_states.shape[1]
    inner_terms = probe_terms + weight_moments(map_states, angles)
    owned_terms = weight_moments(interface_values, angles)
    inner_parts = jnp.moveaxis(
        inner_terms.reshape(2, quad_count, inner_rows // quad_count, 2 * probe_width), 1, 0
    )
    owned_parts = jnp.moveaxis(
        owned_terms.reshape(2, quad_count, owned_rows // quad_count, 2 * probe_width), 1, 0
    )
    both = jnp.concatenate([inner_parts, owned_parts], axis=2).astype(BF16)
    summed_both = lax.all_to_all(both, "quad", split_axis=0, concat_axis=0, tiled=True)
    inner_moments = summed_both[:, :, : inner_rows // quad_count].astype(F32).sum(axis=0)
    owned_moments = summed_both[:, :, inner_rows // quad_count :].astype(F32).sum(axis=0)
    return (inner_moments, owned_moments)


def solution(mesh):
    return jax.shard_map(
        on_device,
        mesh=mesh,
        in_specs=(
            P("quad", None, "area", None),
            P("area", None),
            P("area", None),
            P("area"),
            P(),
            P("area"),
        ),
        out_specs=(P(None, ("area", "quad"), None), P(None, ("area", "quad"), None)),
        check_vma=False,
    )
```

```python
import math

import jax
import jax.numpy as jnp
from jax import lax
from jax.sharding import PartitionSpec as P

ITERS = 4
F32 = jnp.float32
BF16 = jnp.bfloat16


def dot_split(spec, left_parts, right_parts):
    total = None
    for left in left_parts:
        for right in right_parts:
            term = jnp.einsum(spec, left, right, preferred_element_type=F32)
            total = term if total is None else total + term
    return total


def complex_block(values):
    width_half = values.shape[-1] // 2
    value_re = values[..., :width_half]
    value_im = values[..., width_half:]
    lower = jnp.concatenate([-value_im, value_re], axis=-1)
    return jnp.concatenate([values, lower], axis=-2)


def divide_rows(summed, shift_re, shift_im, diagonal_rows):
    width_half = summed.shape[-1] // 2
    real_den = shift_re[:, None] - diagonal_rows[None, :]
    imag_den = shift_im[:, None] * jnp.ones_like(diagonal_rows)[None, :]
    norm_den = real_den * real_den + imag_den * imag_den
    summed_re = summed[..., :width_half]
    summed_im = summed[..., width_half:]
    new_re = (summed_re * real_den[..., None] + summed_im * imag_den[..., None]) / norm_den[
        ..., None
    ]
    new_im = (summed_im * real_den[..., None] - summed_re * imag_den[..., None]) / norm_den[
        ..., None
    ]
    return jnp.concatenate([new_re, new_im], axis=-1)


def sent_and_summed(value, axis, dim):
    before, after = (value.shape[:dim], value.shape[dim + 1 :])
    parts = jnp.moveaxis(value.reshape(*before, lax.axis_size(axis), -1, *after), dim, 0)
    arrived = lax.all_to_all(parts, axis, split_axis=0, concat_axis=0, tiled=True)
    return arrived.sum(axis=0)


def weight_moments(values, angles):
    width_half = values.shape[-1] // 2
    value_re = values[..., :width_half]
    value_im = values[..., width_half:]
    results = []
    for power_index in (1, 2):
        cosine_now = jnp.cos(power_index * angles)[:, None, None]
        sine_now = jnp.sin(power_index * angles)[:, None, None]
        real_term = jnp.sum(cosine_now * value_re - sine_now * value_im, axis=0)
        imag_term = jnp.sum(cosine_now * value_im + sine_now * value_re, axis=0)
        results.append(jnp.concatenate([real_term, imag_term], axis=-1))
    return jnp.stack(results)


def on_device(inverses, coupling, probes, interface_diagonal, area_rows, live_counts):
    local_points = inverses.shape[0]
    area_count = lax.axis_size("area")
    quad_count = lax.axis_size("quad")
    area_index = lax.axis_index("area")
    shared_rows = coupling.shape[1]
    probe_width = probes.shape[1]
    owned_rows = interface_diagonal.shape[0]
    bucket = shared_rows // area_count
    live_mask = jnp.arange(shared_rows) < live_counts[0]
    right = jnp.concatenate([probes, coupling], axis=1)
    applied = jnp.einsum("qrij,jc->qric", inverses, right, preferred_element_type=F32)
    column_mask = jnp.concatenate([jnp.ones((probe_width,), bool), live_mask])
    applied = jnp.where(column_mask, applied, 0.0).astype(BF16)
    row_mask = live_mask[:, None]
    projected_probe = jnp.where(
        row_mask,
        jnp.einsum(
            "ig,qric->qrgc", coupling, applied[..., :probe_width], preferred_element_type=F32
        ),
        0.0,
    )
    projected_map = jnp.where(
        row_mask,
        jnp.einsum(
            "ig,qric->qrgc", coupling, applied[..., probe_width:], preferred_element_type=F32
        ),
        0.0,
    )
    probe_state = jnp.concatenate(
        [applied[:, 0, :, :probe_width], applied[:, 1, :, :probe_width]], axis=-1
    )
    reply_start = jnp.concatenate([projected_probe[:, 0], projected_probe[:, 1]], axis=-1)
    reply_map = jnp.concatenate([projected_map[:, 0], projected_map[:, 1]], axis=-1)
    reply_parts = (reply_map.astype(BF16),)
    block_offsets = (
        lax.dynamic_slice_in_dim(area_rows, area_index * bucket, bucket, 1)
        - area_index * owned_rows
    )
    flat_offsets = block_offsets.reshape(-1)
    selector = (flat_offsets[None, :] == jnp.arange(owned_rows)[:, None]).astype(BF16)
    selector = selector.reshape(owned_rows, area_count, bucket)
    angle_step = jnp.float32(2.0 * math.pi / (local_points * quad_count))
    point_ids = lax.axis_index("quad") * local_points + jnp.arange(local_points, dtype=jnp.int32)
    angles = (point_ids.astype(jnp.float32) + 0.5) * angle_step
    shift_re = jnp.cos(angles)
    shift_im = jnp.sin(angles)
    gathered_block = None
    interface_values = None
    for sweep_index in range(ITERS):
        if sweep_index == 0:
            replies = reply_start
        else:
            replies = reply_start + dot_split("qgh,qhc->qgc", reply_parts, (gathered_block,))
        parcels = jnp.moveaxis(
            replies.reshape(local_points, area_count, bucket, 2 * probe_width), 1, 0
        ).astype(BF16)
        arrived = lax.all_to_all(parcels, "area", split_axis=0, concat_axis=0, tiled=True)
        summed = jnp.einsum("rbs,bqsc->qrc", selector, arrived, preferred_element_type=F32)
        interface_values = divide_rows(summed, shift_re, shift_im, interface_diagonal)
        outgoing = jnp.einsum(
            "rbs,qrc->bqsc",
            selector,
            interface_values.astype(BF16),
            preferred_element_type=F32,
        ).astype(BF16)
        returned = lax.all_to_all(outgoing, "area", split_axis=0, concat_axis=0, tiled=True)
        gathered_rows = jnp.moveaxis(returned, 0, 1).reshape(
            local_points, shared_rows, 2 * probe_width
        )
        gathered_block = complex_block(gathered_rows)
    part_block = gathered_block.reshape(local_points, 2, shared_rows, 2 * probe_width)
    states = probe_state.astype(F32) + jnp.einsum(
        "qris,qrsc->qic", applied[..., probe_width:], part_block, preferred_element_type=F32
    )
    inner_rows = states.shape[1]
    inner_terms = weight_moments(states, angles)
    owned_terms = weight_moments(interface_values, angles)
    inner_parts = jnp.moveaxis(
        inner_terms.reshape(2, quad_count, inner_rows // quad_count, 2 * probe_width), 1, 0
    )
    owned_parts = jnp.moveaxis(
        owned_terms.reshape(2, quad_count, owned_rows // quad_count, 2 * probe_width), 1, 0
    )
    both = jnp.concatenate([inner_parts, owned_parts], axis=2).astype(BF16)
    summed_both = lax.all_to_all(both, "quad", split_axis=0, concat_axis=0, tiled=True)
    inner_moments = summed_both[:, :, : inner_rows // quad_count].astype(F32).sum(axis=0)
    owned_moments = summed_both[:, :, inner_rows // quad_count :].astype(F32).sum(axis=0)
    return (inner_moments, owned_moments)


def solution(mesh):
    return jax.shard_map(
        on_device,
        mesh=mesh,
        in_specs=(
            P("quad", None, "area", None),
            P("area", None),
            P("area", None),
            P("area"),
            P(),
            P("area"),
        ),
        out_specs=(P(None, ("area", "quad"), None), P(None, ("area", "quad"), None)),
        check_vma=False,
    )
```
